32 devices in a mesh: tile: 4 (over x, core), mem: 8 (over z, y).
Axes of the slice: x: 2, y: 2, z: 4, core: 2. Of those that a mesh axis runs over, the one named last changes fastest.
Arguments:
- perturbations: bfloat16 [32, 2, 16, 16, 512], P('mem', None, 'tile'), may hold values from -3 to 3
- innovations: float32 [4, 32768], P('tile', 'mem'), may hold values from -6 to 6
- obs_weight: float32 [4, 32768], P('tile', 'mem'), may hold values from 0.4 to 4
- obs_cell: int32 [4, 32768], P('tile', 'mem'), may hold values from 0 to 8191
- row_start: int32 [16], P('tile'), may hold values from 0 to 511
- row_length: int32 [16], P('tile'), may hold values from 256 to 512
- lat_rate: float32 [16], replicated, may hold values from 0.3 to 0.4
- lon_rate: float32 [16], replicated, may hold values from 0.02 to 0.1
Outputs:
- control: float32 [32, 16, 16, 512], P('mem', 'tile')
- increment: float32 [2, 16, 8192], P(None, 'tile', 'mem')
The draws below stay inside these ranges and needn't reach their ends.
All inputs are finite; a program needn't handle non-finite values.
Results may differ from the reference program's by a relative error of at most 0.0003.
Values sent between devices are 32-bit elements; how exact they have to be, the bound alone decides.
No kernel may reach another device: no remote copies, remote signals or barrier semaphores. Data moves between devices by JAX's collectives and lax.ppermute only.
A program may use at most 64 MiB of HBM per device.

```python
import math
import jax
import jax.numpy as jnp
from jax import lax

MEMBERS = 32
NLON = 512
LEV = 16
SLOTS = 2
ITERS = 2
STEPS = 8
LAT_TILE = 4
OBS_DEV = 4096
NLAT = 16
N_TILE = 4
N_MEM = 8


def set_ends(values, stream_key, low, high):
    longest = values.shape.index(max(values.shape))
    spots = []
    for shift in (0, 1):
        where = [jax.random.randint(jax.random.fold_in(stream_key, axis), (), 0, length) for axis, length in enumerate(values.shape)]
        where[longest] = (where[longest] + shift) % values.shape[longest]
        spots.append(tuple(where))
    return values.at[spots[0]].set(low).at[spots[1]].set(high)


def level_of(own_key, extent, shards, smallest, top_value):
    factor_of = 1.0
    for position, shards_of in shards:
        heights = jax.random.uniform(jax.random.fold_in(jax.random.fold_in(own_key, 6), position), (shards_of,), jnp.float32, smallest / len(shards), top_value / len(shards))
        factor_of = factor_of * jnp.repeat(jnp.exp(heights), extent[position] // shards_of).reshape((-1,) + (1,) * (len(extent) - 1 - position))
    return factor_of


def scatter_about(stream_key, dims, width, limit, pieces=(), kind=jnp.bfloat16):
    drawn = width * jax.random.normal(stream_key, dims, jnp.float32)
    if pieces:
        drawn = drawn * level_of(stream_key, dims, pieces, -0.22, 0.18)
    return jnp.clip(drawn, -limit, limit).astype(kind)


def setup_inputs(seed: int = 0) -> dict:
    seeds = jax.random.split(jax.random.key(seed), 9)
    return {
        "perturbations": scatter_about(seeds[0], (MEMBERS, SLOTS, NLAT, LEV, NLON), 0.5, 3.0, ((0, 8), (2, 4))),
        "innovations": scatter_about(seeds[1], (N_TILE, N_MEM * OBS_DEV), 1.0, 6.0, ((0, 4), (1, 8)), jnp.float32),
        "obs_weight": jnp.clip(jnp.exp(math.log(4.0) - 2.3025851 * jax.random.uniform(seeds[2], (N_TILE, N_MEM * OBS_DEV), jnp.float32) ** level_of(seeds[2], (N_TILE, N_MEM * OBS_DEV), ((0, 4), (1, 8)), -0.2, 0.2)), 0.4, 4.0),
        "obs_cell": set_ends(jax.random.randint(seeds[3], (N_TILE, N_MEM * OBS_DEV), 0, SLOTS * LAT_TILE * LEV * NLON // N_MEM), jax.random.fold_in(seeds[3], 1), 0, (SLOTS * LAT_TILE * LEV * NLON // N_MEM) - 1).astype(jnp.int32),
        "row_start": set_ends(jax.random.randint(seeds[4], (NLAT,), 0, NLON), jax.random.fold_in(seeds[4], 1), 0, NLON - 1).astype(jnp.int32),
        "row_length": set_ends(jax.random.randint(seeds[5], (NLAT,), NLON // 2, NLON + 1), jax.random.fold_in(seeds[5], 1), NLON // 2, NLON).astype(jnp.int32),
        "lat_rate": jnp.clip(jax.random.uniform(seeds[6], (LEV,), jnp.float32, 0.3, 0.4), 0.3, 0.4),
        "lon_rate": jnp.clip(jax.random.uniform(seeds[7], (LEV,), jnp.float32, 0.02, 0.1), 0.02, 0.1),
    }


def row_mask(starts, lengths, nlon):
    lon = lax.broadcasted_iota(jnp.int32, (starts.shape[0], nlon), 1)
    rel = (lon - starts[:, None]) % nlon
    return jnp.where(rel < lengths[:, None], 1.0, 0.0).astype(jnp.float32)[:, None, :]


def diffuse_step(field, mask, lat_rate, lon_rate):
    zero = jnp.zeros_like(field[:, :1])
    north = jnp.concatenate([field[:, 1:], zero], axis=1)
    south = jnp.concatenate([zero, field[:, :-1]], axis=1)
    east = jnp.roll(field, -1, axis=3)
    west = jnp.roll(field, 1, axis=3)
    lat_term = north + south - 2.0 * field
    lon_term = east + west - 2.0 * field
    return mask * (field + lat_rate[:, None] * lat_term + lon_rate[:, None] * lon_term)


def reference(perturbations, innovations, obs_weight, obs_cell, row_start, row_length, lat_rate, lon_rate):
    mask = row_mask(row_start, row_length, NLON)
    cols = LEV * NLON
    shard_cols = cols // N_MEM

    def smooth(field):
        current = mask * field
        for inner in range(STEPS):
            current = diffuse_step(current, mask, lat_rate, lon_rate)
        return current

    def forward(control):
        smoothed = smooth(control)
        summed = jnp.sum(perturbations * smoothed[:, None], axis=0)
        return summed.reshape(SLOTS, NLAT, cols)

    def adjoint(gradient):
        field = gradient.reshape(SLOTS, NLAT, LEV, NLON)
        return smooth(jnp.sum(perturbations * field[None], axis=1))

    tile_idx = lax.broadcasted_iota(jnp.int32, obs_cell.shape, 0)
    block = lax.broadcasted_iota(jnp.int32, obs_cell.shape, 1) // OBS_DEV
    block_row = obs_cell // shard_cols
    slot = block_row // LAT_TILE
    lat = block_row % LAT_TILE
    positions = ((slot * NLAT + tile_idx * LAT_TILE + lat) * cols + block * shard_cols + obs_cell % shard_cols).reshape(-1)
    weight = obs_weight.reshape(-1)
    innov = innovations.reshape(-1)

    def grid_of(values):
        return jnp.zeros((SLOTS * NLAT * cols,), jnp.float32).at[positions].add(values).reshape(SLOTS, NLAT, cols)

    def observe_back(state):
        return grid_of(weight * state.reshape(-1)[positions])

    residual = adjoint(grid_of(weight * innov))
    direction = residual
    control = jnp.zeros_like(residual)
    increment = jnp.zeros((SLOTS, NLAT, cols), jnp.float32)
    norm_now = jnp.sum(residual * residual)
    for step in range(ITERS):
        state = forward(direction)
        image = direction + adjoint(observe_back(state))
        alpha = norm_now / jnp.sum(direction * image)
        control = control + alpha * direction
        increment = increment + alpha * state
        if step + 1 < ITERS:
            residual = residual - alpha * image
            norm_next = jnp.sum(residual * residual)
            direction = residual + (norm_next / norm_now) * direction
            norm_now = norm_next
    return control, increment
```

```python
import jax
import jax.numpy as jnp
from jax import lax
from jax.sharding import PartitionSpec as P

ITERS = 2
STEPS = 8
DEPTH = 4


def with_halo(block, sides, width):
    for axis, dim in sides:
        count = lax.axis_size(axis)
        forward = [(i, i + 1) for i in range(count - 1)]
        backward = [(target, source) for source, target in forward]
        low = lax.ppermute(
            lax.slice_in_dim(block, block.shape[dim] - width, None, axis=dim), axis, forward
        )
        high = lax.ppermute(lax.slice_in_dim(block, 0, width, axis=dim), axis, backward)
        block = jnp.concatenate([low, block, high], axis=dim)
    return block


def row_mask(starts, lengths, nlon):
    lon = lax.broadcasted_iota(jnp.int32, (starts.shape[0], nlon), 1)
    rel = (lon - starts[:, None]) % nlon
    return jnp.where(rel < lengths[:, None], 1.0, 0.0).astype(jnp.float32)[:, None, :]


def diffuse_step(field, mask, lat_rate, lon_rate):
    zero = jnp.zeros_like(field[:, :1])
    north = jnp.concatenate([field[:, 1:], zero], axis=1)
    south = jnp.concatenate([zero, field[:, :-1]], axis=1)
    east = jnp.roll(field, -1, axis=3)
    west = jnp.roll(field, 1, axis=3)
    lat_term = north + south - 2.0 * field
    lon_term = east + west - 2.0 * field
    return mask * (
        field + lat_rate[:, None, None, None] * lat_term + lon_rate[:, None, None, None] * lon_term
    )


def global_sum(value):
    return lax.psum(value, ("tile", "mem"))


def body(
    perturbations, innovations, obs_weight, obs_cell, row_start, row_length, lat_rate, lon_rate
):
    slots = perturbations.shape[1]
    lat_rows = perturbations.shape[2]
    levels = perturbations.shape[3]
    nlon = perturbations.shape[4]
    groups = lax.axis_size("mem")
    own_levels = levels // groups
    shard_cols = own_levels * nlon
    first = lax.axis_index("mem") * own_levels
    lat_own = lax.dynamic_slice_in_dim(lat_rate, first, own_levels)
    lon_own = lax.dynamic_slice_in_dim(lon_rate, first, own_levels)

    pert = lax.all_to_all(
        perturbations.astype(jnp.float32).transpose(1, 3, 2, 0, 4),
        "mem",
        split_axis=1,
        concat_axis=3,
        tiled=True,
    )

    own_mask = row_mask(row_start, row_length, nlon)
    tables = with_halo(jnp.stack([row_start, row_length]), (("tile", 1),), DEPTH)
    wide_mask = row_mask(tables[0], tables[1], nlon)

    def smooth(field):
        current = own_mask * field
        for block in range(STEPS // DEPTH):
            wide = with_halo(current, (("tile", 1),), DEPTH)
            for inner in range(DEPTH):
                wide = diffuse_step(wide, wide_mask, lat_own, lon_own)
            current = wide[:, DEPTH : DEPTH + lat_rows]
        return current

    def forward(control):
        smoothed = smooth(control)
        return jnp.sum(pert * smoothed[None], axis=3)

    def adjoint(gradient):
        return smooth(jnp.sum(pert * gradient[:, :, :, None], axis=0))

    local_cells = obs_cell[0]
    innov = innovations[0]
    weight = obs_weight[0]
    size = slots * lat_rows * shard_cols
    state_shape = (slots, own_levels, lat_rows, nlon)
    gathered = jnp.zeros((size, 2), jnp.float32).at[local_cells].add(
        jnp.stack([weight * innov, weight], axis=1)
    )
    gathered = gathered.reshape(slots, lat_rows, own_levels, nlon, 2).transpose(4, 0, 2, 1, 3)
    first_grad = gathered[0]
    obs_diag = gathered[1]

    residual = adjoint(first_grad)
    direction = residual
    control = jnp.zeros_like(residual)
    increment = jnp.zeros(state_shape, jnp.float32)
    norm_now = global_sum(jnp.sum(residual * residual))
    for step in range(ITERS):
        state = forward(direction)
        image = direction + adjoint(obs_diag * state)
        alpha = norm_now / global_sum(jnp.sum(direction * image))
        control = control + alpha * direction
        increment = increment + alpha * state
        if step + 1 < ITERS:
            residual = residual - alpha * image
            norm_next = global_sum(jnp.sum(residual * residual))
            direction = residual + norm_next / norm_now * direction
            norm_now = norm_next
    control = lax.all_to_all(control, "mem", split_axis=2, concat_axis=0, tiled=True)
    control = control.transpose(2, 1, 0, 3)
    increment = increment.transpose(0, 2, 1, 3).reshape(slots, lat_rows, shard_cols)
    return (control, increment)


def solution(mesh):
    return jax.shard_map(
        body,
        mesh=mesh,
        in_specs=(
            P("mem", None, "tile", None, None),
            P("tile", "mem"),
            P("tile", "mem"),
            P("tile", "mem"),
            P("tile"),
            P("tile"),
            P(),
            P(),
        ),
        out_specs=(P("mem", "tile", None, None), P(None, "tile", "mem")),
        check_vma=False,
    )
```

```python
import jax
import jax.numpy as jnp
from jax import lax
from jax.sharding import PartitionSpec as P

ITERS = 2
STEPS = 8


def with_halo(block, axis, dim, width):
    count = lax.axis_size(axis)
    rows = block.shape[dim]
    hops = -(-width // rows)
    lows, highs = [], []
    for hop in range(hops, 0, -1):
        forward = [(i, i + hop) for i in range(count - hop)]
        lows.append(lax.ppermute(block, axis, forward))
    for hop in range(1, hops + 1):
        backward = [(i + hop, i) for i in range(count - hop)]
        highs.append(lax.ppermute(block, axis, backward))
    low = jnp.concatenate(lows, axis=dim) if hops > 1 else lows[0]
    high = jnp.concatenate(highs, axis=dim) if hops > 1 else highs[0]
    low = lax.slice_in_dim(low, low.shape[dim] - width, None, axis=dim)
    high = lax.slice_in_dim(high, 0, width, axis=dim)
    return jnp.concatenate([low, block, high], axis=dim)


def row_mask(starts, lengths, nlon):
    lon = lax.broadcasted_iota(jnp.int32, (starts.shape[0], nlon), 1)
    rel = (lon - starts[:, None]) % nlon
    return jnp.where(rel < lengths[:, None], 1.0, 0.0).astype(jnp.float32)[:, None, :]


def diffuse_step(field, mask, lat_rate, lon_rate):
    centre = field[:, 1:-1]
    north = field[:, 2:]
    south = field[:, :-2]
    east = jnp.roll(centre, -1, axis=3)
    west = jnp.roll(centre, 1, axis=3)
    lat_term = north + south - 2.0 * centre
    lon_term = east + west - 2.0 * centre
    return mask * (
        centre + lat_rate[:, None, None, None] * lat_term + lon_rate[:, None, None, None] * lon_term
    )


def global_sum(value):
    axes = ("tile", "mem")
    count = lax.axis_size(axes)
    spread = jnp.broadcast_to(value.astype(jnp.float32), (count,))
    return jnp.sum(lax.all_to_all(spread, axes, 0, 0, tiled=True))


def body(
    perturbations, innovations, obs_weight, obs_cell, row_start, row_length, lat_rate, lon_rate
):
    slots = perturbations.shape[1]
    lat_rows = perturbations.shape[2]
    levels = perturbations.shape[3]
    nlon = perturbations.shape[4]
    groups = lax.axis_size("mem")
    own_levels = levels // groups
    shard_cols = own_levels * nlon
    first = lax.axis_index("mem") * own_levels
    lat_own = lax.dynamic_slice_in_dim(lat_rate, first, own_levels)
    lon_own = lax.dynamic_slice_in_dim(lon_rate, first, own_levels)

    pert = lax.all_to_all(
        perturbations.astype(jnp.float32).transpose(1, 3, 2, 0, 4),
        "mem",
        split_axis=1,
        concat_axis=3,
        tiled=True,
    )

    own_mask = row_mask(row_start, row_length, nlon)
    tables = with_halo(jnp.stack([row_start, row_length]), "tile", 1, STEPS)
    wide_mask = row_mask(tables[0], tables[1], nlon)

    def smooth(field):
        wide = with_halo(own_mask * field, "tile", 1, STEPS)
        for inner in range(STEPS):
            keep = wide_mask[inner + 1 : wide_mask.shape[0] - inner - 1]
            wide = diffuse_step(wide, keep, lat_own, lon_own)
        return wide

    def forward(control):
        smoothed = smooth(control)
        return jnp.sum(pert * smoothed[None], axis=3)

    def adjoint(gradient):
        return smooth(jnp.sum(pert * gradient[:, :, :, None], axis=0))

    local_cells = obs_cell[0]
    innov = innovations[0]
    weight = obs_weight[0]
    size = slots * lat_rows * shard_cols
    state_shape = (slots, own_levels, lat_rows, nlon)
    gathered = jnp.zeros((size, 2), jnp.float32).at[local_cells].add(
        jnp.stack([weight * innov, weight], axis=1)
    )
    gathered = gathered.reshape(slots, lat_rows, own_levels, nlon, 2).transpose(4, 0, 2, 1, 3)
    first_grad = gathered[0]
    obs_diag = gathered[1]

    residual = adjoint(first_grad)
    direction = residual
    control = jnp.zeros_like(residual)
    increment = jnp.zeros(state_shape, jnp.float32)
    norm_now = global_sum(jnp.sum(residual * residual))
    for step in range(ITERS):
        state = forward(direction)
        image = direction + adjoint(obs_diag * state)
        alpha = norm_now / global_sum(jnp.sum(direction * image))
        control = control + alpha * direction
        increment = increment + alpha * state
        if step + 1 < ITERS:
            residual = residual - alpha * image
            norm_next = global_sum(jnp.sum(residual * residual))
            direction = residual + norm_next / norm_now * direction
            norm_now = norm_next
    control = lax.all_to_all(control, "mem", split_axis=2, concat_axis=0, tiled=True)
    control = control.transpose(2, 1, 0, 3)
    increment = increment.transpose(0, 2, 1, 3).reshape(slots, lat_rows, shard_cols)
    return (control, increment)


def solution(mesh):
    return jax.shard_map(
        body,
        mesh=mesh,
        in_specs=(
            P("mem", None, "tile", None, None),
            P("tile", "mem"),
            P("tile", "mem"),
            P("tile", "mem"),
            P("tile"),
            P("tile"),
            P(),
            P(),
        ),
        out_specs=(P("mem", "tile", None, None), P(None, "tile", "mem")),
        check_vma=False,
    )
```

```python
import jax
import jax.numpy as jnp
from jax import lax
from jax.sharding import PartitionSpec as P

ITERS = 2
STEPS = 8


def row_mask(starts, lengths, nlon):
    lon = lax.broadcasted_iota(jnp.int32, (starts.shape[0], nlon), 1)
    rel = (lon - starts[:, None]) % nlon
    return jnp.where(rel < lengths[:, None], 1.0, 0.0).astype(jnp.float32)[:, None, :]


def diffuse_step(field, mask, lat_rate, lon_rate):
    zero = jnp.zeros_like(field[:, :1])
    north = jnp.concatenate([field[:, 1:], zero], axis=1)
    south = jnp.concatenate([zero, field[:, :-1]], axis=1)
    east = jnp.roll(field, -1, axis=3)
    west = jnp.roll(field, 1, axis=3)
    lat_term = north + south - 2.0 * field
    lon_term = east + west - 2.0 * field
    return mask * (
        field + lat_rate[:, None, None, None] * lat_term + lon_rate[:, None, None, None] * lon_term
    )


def global_sum(value):
    axes = ("tile", "mem")
    count = lax.axis_size(axes)
    spread = jnp.broadcast_to(value.astype(jnp.float32), (count,))
    return jnp.sum(lax.all_to_all(spread, axes, 0, 0, tiled=True))


def gather_rows(block, dim):
    count = lax.axis_size("tile")
    shape = block.shape
    copies = jnp.broadcast_to(
        jnp.expand_dims(block, dim), shape[:dim] + (count,) + shape[dim:]
    )
    joined = lax.all_to_all(copies, "tile", dim, dim, tiled=True)
    return joined.reshape(shape[:dim] + (count * shape[dim],) + shape[dim + 1 :])


def reduce_rows(block, dim):
    count = lax.axis_size("tile")
    shape = block.shape
    parts = block.reshape(shape[:dim] + (count, shape[dim] // count) + shape[dim + 1 :])
    received = lax.all_to_all(parts, "tile", dim, dim, tiled=True)
    return jnp.sum(received, axis=dim)


def body(
    perturbations, innovations, obs_weight, obs_cell, row_start, row_length, lat_rate, lon_rate
):
    slots = perturbations.shape[1]
    lat_rows = perturbations.shape[2]
    levels = perturbations.shape[3]
    nlon = perturbations.shape[4]
    groups = lax.axis_size("mem")
    own_levels = levels // groups
    shard_cols = own_levels * nlon
    first = lax.axis_index("mem") * own_levels
    lat_own = lax.dynamic_slice_in_dim(lat_rate, first, own_levels)
    lon_own = lax.dynamic_slice_in_dim(lon_rate, first, own_levels)

    pert = lax.all_to_all(
        perturbations.astype(jnp.float32).transpose(1, 3, 2, 0, 4),
        "mem",
        split_axis=1,
        concat_axis=3,
        tiled=True,
    )
    pert = lax.all_to_all(pert, "tile", split_axis=3, concat_axis=2, tiled=True)

    tables = gather_rows(jnp.stack([row_start, row_length]), 1)
    mask = row_mask(tables[0], tables[1], nlon)

    def smooth(field):
        current = mask * field
        for inner in range(STEPS):
            current = diffuse_step(current, mask, lat_own, lon_own)
        return current

    def forward(control):
        smoothed = smooth(control)
        return reduce_rows(jnp.sum(pert * smoothed[None], axis=3), 2)

    def adjoint(gradient):
        return smooth(jnp.sum(pert * gradient[:, :, :, None], axis=0))

    local_cells = obs_cell[0]
    innov = innovations[0]
    weight = obs_weight[0]
    size = slots * lat_rows * shard_cols
    state_shape = (slots, own_levels, lat_rows, nlon)
    gathered = jnp.zeros((size, 2), jnp.float32).at[local_cells].add(
        jnp.stack([weight * innov, weight], axis=1)
    )
    gathered = gathered.reshape(slots, lat_rows, own_levels, nlon, 2).transpose(4, 0, 2, 1, 3)
    obs_diag = gathered[1]

    residual = adjoint(gather_rows(gathered[0], 2))
    direction = residual
    control = jnp.zeros_like(residual)
    increment = jnp.zeros(state_shape, jnp.float32)
    norm_now = global_sum(jnp.sum(residual * residual))
    for step in range(ITERS):
        state = forward(direction)
        image = direction + adjoint(gather_rows(obs_diag * state, 2))
        alpha = norm_now / global_sum(jnp.sum(direction * image))
        control = control + alpha * direction
        increment = increment + alpha * state
        if step + 1 < ITERS:
            residual = residual - alpha * image
            norm_next = global_sum(jnp.sum(residual * residual))
            direction = residual + norm_next / norm_now * direction
            norm_now = norm_next
    control = lax.all_to_all(control, "tile", split_axis=1, concat_axis=2, tiled=True)
    control = lax.all_to_all(control, "mem", split_axis=2, concat_axis=0, tiled=True)
    control = control.transpose(2, 1, 0, 3)
    increment = increment.transpose(0, 2, 1, 3).reshape(slots, lat_rows, shard_cols)
    return (control, increment)


def solution(mesh):
    return jax.shard_map(
        body,
        mesh=mesh,
        in_specs=(
            P("mem", None, "tile", None, None),
            P("tile", "mem"),
            P("tile", "mem"),
            P("tile", "mem"),
            P("tile"),
            P("tile"),
            P(),
            P(),
        ),
        out_specs=(P("mem", "tile", None, None), P(None, "tile", "mem")),
        check_vma=False,
    )
```

```python
import jax
import jax.numpy as jnp
from jax import lax
from jax.sharding import PartitionSpec as P

ITERS = 2
STEPS = 8


def row_mask(starts, lengths, nlon):
    lon = lax.broadcasted_iota(jnp.int32, (starts.shape[0], nlon), 1)
    rel = (lon - starts[:, None]) % nlon
    return jnp.where(rel < lengths[:, None], 1.0, 0.0).astype(jnp.float32)[:, None, :]


def diffuse_step(field, mask, lat_rate, lon_rate):
    zero = jnp.zeros_like(field[:, :1])
    north = jnp.concatenate([field[:, 1:], zero], axis=1)
    south = jnp.concatenate([zero, field[:, :-1]], axis=1)
    east = jnp.roll(field, -1, axis=3)
    west = jnp.roll(field, 1, axis=3)
    lat_term = north + south - 2.0 * field
    lon_term = east + west - 2.0 * field
    return mask * (
        field + lat_rate[:, None, None, None] * lat_term + lon_rate[:, None, None, None] * lon_term
    )


def global_sum(value):
    axes = ("tile", "mem")
    count = lax.axis_size(axes)
    value = jnp.asarray(value, jnp.float32)
    spread = jnp.broadcast_to(value, (count,) + value.shape)
    return jnp.sum(lax.all_to_all(spread, axes, 0, 0, tiled=True), axis=0)


def add_at_cells(cells, values, size):
    lanes = 128
    count, kinds = values.shape
    high = lax.broadcasted_iota(jnp.int32, (count, size // lanes), 1) == (cells // lanes)[:, None]
    low = lax.broadcasted_iota(jnp.int32, (count, lanes), 1) == (cells % lanes)[:, None]
    spread = values[:, :, None] * low.astype(jnp.float32)[:, None, :]
    summed = jnp.dot(
        high.astype(jnp.float32).T,
        spread.reshape(count, kinds * lanes),
        precision=lax.Precision.HIGHEST,
        preferred_element_type=jnp.float32,
    )
    return summed.reshape(size // lanes, kinds, lanes).transpose(0, 2, 1).reshape(size, kinds)


def gather_rows(block, dim):
    count = lax.axis_size("tile")
    shape = block.shape
    copies = jnp.broadcast_to(
        jnp.expand_dims(block, dim), shape[:dim] + (count,) + shape[dim:]
    )
    joined = lax.all_to_all(copies, "tile", dim, dim, tiled=True)
    return joined.reshape(shape[:dim] + (count * shape[dim],) + shape[dim + 1 :])


def reduce_rows(block, dim):
    count = lax.axis_size("tile")
    shape = block.shape
    parts = block.reshape(shape[:dim] + (count, shape[dim] // count) + shape[dim + 1 :])
    received = lax.all_to_all(parts, "tile", dim, dim, tiled=True)
    return jnp.sum(received, axis=dim)


def body(
    perturbations, innovations, obs_weight, obs_cell, row_start, row_length, lat_rate, lon_rate
):
    slots = perturbations.shape[1]
    lat_rows = perturbations.shape[2]
    levels = perturbations.shape[3]
    nlon = perturbations.shape[4]
    groups = lax.axis_size("mem")
    own_levels = levels // groups
    shard_cols = own_levels * nlon
    first = lax.axis_index("mem") * own_levels
    lat_own = lax.dynamic_slice_in_dim(lat_rate, first, own_levels)
    lon_own = lax.dynamic_slice_in_dim(lon_rate, first, own_levels)

    tiles = lax.axis_size("tile")
    local_members = perturbations.shape[0]
    share = local_members // tiles
    if share and local_members % tiles == 0:
        sent = perturbations.astype(jnp.float32).reshape(
            tiles, share, slots, lat_rows, groups, own_levels, nlon
        )
        sent = sent.transpose(0, 4, 2, 5, 3, 1, 6).reshape(
            tiles * groups, slots, own_levels, lat_rows, share, nlon
        )
        got = lax.all_to_all(sent, ("tile", "mem"), 0, 0, tiled=True)
        pert = got.reshape(tiles, groups, slots, own_levels, lat_rows, share, nlon)
        pert = pert.transpose(2, 3, 0, 4, 1, 5, 6).reshape(
            slots, own_levels, tiles * lat_rows, groups * share, nlon
        )
    else:
        pert = lax.all_to_all(
            perturbations.astype(jnp.float32).transpose(1, 3, 2, 0, 4),
            "mem",
            split_axis=1,
            concat_axis=3,
            tiled=True,
        )
        pert = lax.all_to_all(pert, "tile", split_axis=3, concat_axis=2, tiled=True)

    def smooth(field):
        current = mask * field
        for inner in range(STEPS):
            current = diffuse_step(current, mask, lat_own, lon_own)
        return current

    def forward(control):
        smoothed = smooth(control)
        return reduce_rows(jnp.sum(pert * smoothed[None], axis=3), 2)

    def adjoint(gradient):
        return smooth(jnp.sum(pert * gradient[:, :, :, None], axis=0))

    local_cells = obs_cell[0]
    innov = innovations[0]
    weight = obs_weight[0]
    size = slots * lat_rows * shard_cols
    state_shape = (slots, own_levels, lat_rows, nlon)
    gathered = add_at_cells(local_cells, jnp.stack([weight * innov, weight], axis=1), size)
    gathered = gathered.reshape(slots, lat_rows, own_levels, nlon, 2).transpose(4, 0, 2, 1, 3)
    obs_diag = gathered[1]

    tables = jnp.zeros((lat_rows, nlon), jnp.float32)
    tables = tables.at[:, 0].set(row_start.astype(jnp.float32))
    tables = tables.at[:, 1].set(row_length.astype(jnp.float32))
    payload = jnp.concatenate(
        [gathered[0].reshape(slots * own_levels, lat_rows, nlon), tables[None]], axis=0
    )
    payload = gather_rows(payload, 1)
    tables = payload[-1, :, :2].astype(jnp.int32)
    mask = row_mask(tables[:, 0], tables[:, 1], nlon)
    first_grad = payload[:-1].reshape(slots, own_levels, tiles * lat_rows, nlon)

    residual = adjoint(first_grad)
    direction = residual
    control = jnp.zeros_like(residual)
    increment = jnp.zeros(state_shape, jnp.float32)
    norm_now = None
    for step in range(ITERS):
        state = forward(direction)
        image = direction + adjoint(gather_rows(obs_diag * state, 2))
        if norm_now is None:
            sums = global_sum(jnp.stack([jnp.sum(residual * residual), jnp.sum(direction * image)]))
            norm_now, curvature = sums[0], sums[1]
        else:
            curvature = global_sum(jnp.sum(direction * image))
        alpha = norm_now / curvature
        control = control + alpha * direction
        increment = increment + alpha * state
        if step + 1 < ITERS:
            residual = residual - alpha * image
            norm_next = global_sum(jnp.sum(residual * residual))
            direction = residual + norm_next / norm_now * direction
            norm_now = norm_next
    if share and local_members % tiles == 0:
        sent = control.reshape(own_levels, tiles, lat_rows, groups, share, nlon)
        sent = sent.transpose(1, 3, 0, 2, 4, 5).reshape(
            tiles * groups, own_levels, lat_rows, share, nlon
        )
        got = lax.all_to_all(sent, ("tile", "mem"), 0, 0, tiled=True)
        control = got.reshape(tiles, groups, own_levels, lat_rows, share, nlon)
        control = control.transpose(0, 4, 3, 1, 2, 5).reshape(
            tiles * share, lat_rows, levels, nlon
        )
    else:
        control = lax.all_to_all(control, "tile", split_axis=1, concat_axis=2, tiled=True)
        control = lax.all_to_all(control, "mem", split_axis=2, concat_axis=0, tiled=True)
        control = control.transpose(2, 1, 0, 3)
    increment = increment.transpose(0, 2, 1, 3).reshape(slots, lat_rows, shard_cols)
    return (control, increment)


def solution(mesh):
    return jax.shard_map(
        body,
        mesh=mesh,
        in_specs=(
            P("mem", None, "tile", None, None),
            P("tile", "mem"),
            P("tile", "mem"),
            P("tile", "mem"),
            P("tile"),
            P("tile"),
            P(),
            P(),
        ),
        out_specs=(P("mem", "tile", None, None), P(None, "tile", "mem")),
        check_vma=False,
    )
```

```python
import jax
import jax.numpy as jnp
from jax import lax
from jax.sharding import PartitionSpec as P

ITERS = 2
STEPS = 8


def row_mask(starts, lengths, nlon):
    lon = lax.broadcasted_iota(jnp.int32, (starts.shape[0], nlon), 1)
    rel = (lon - starts[:, None]) % nlon
    return jnp.where(rel < lengths[:, None], 1.0, 0.0).astype(jnp.float32)[:, None, :]


def diffuse_step(field, mask, lat_rate, lon_rate):
    zero = jnp.zeros_like(field[:, :1])
    north = jnp.concatenate([field[:, 1:], zero], axis=1)
    south = jnp.concatenate([zero, field[:, :-1]], axis=1)
    east = jnp.roll(field, -1, axis=3)
    west = jnp.roll(field, 1, axis=3)
    lat_term = north + south - 2.0 * field
    lon_term = east + west - 2.0 * field
    return mask * (
        field + lat_rate[:, None, None, None] * lat_term + lon_rate[:, None, None, None] * lon_term
    )


def global_sum(value):
    axes = ("tile", "mem")
    count = lax.axis_size(axes)
    value = jnp.asarray(value, jnp.float32)
    spread = jnp.broadcast_to(value, (count,) + value.shape)
    return jnp.sum(lax.all_to_all(spread, axes, 0, 0, tiled=True), axis=0)


def add_at_cells(cells, values, size):
    lanes = 128
    count, kinds = values.shape
    high = lax.broadcasted_iota(jnp.int32, (count, size // lanes), 1) == (cells // lanes)[:, None]
    low = lax.broadcasted_iota(jnp.int32, (count, lanes), 1) == (cells % lanes)[:, None]
    spread = values[:, :, None] * low.astype(jnp.float32)[:, None, :]
    summed = jnp.dot(
        high.astype(jnp.float32).T,
        spread.reshape(count, kinds * lanes),
        precision=lax.Precision.HIGHEST,
        preferred_element_type=jnp.float32,
    )
    return summed.reshape(size // lanes, kinds, lanes).transpose(0, 2, 1).reshape(size, kinds)


def gather_rows(block, dim):
    count = lax.axis_size("tile")
    shape = block.shape
    copies = jnp.broadcast_to(
        jnp.expand_dims(block, dim), shape[:dim] + (count,) + shape[dim:]
    )
    joined = lax.all_to_all(copies, "tile", dim, dim, tiled=True)
    return joined.reshape(shape[:dim] + (count * shape[dim],) + shape[dim + 1 :])


def gather_rows_by_permutes(block, dim):
    count = lax.axis_size("tile")
    me = lax.axis_index("tile")
    pieces = [block] + [
        lax.ppermute(block, "tile", [(i, (i + k) % count) for i in range(count)])
        for k in range(1, count)
    ]
    by_offset = jnp.stack([pieces[(count - q) % count] for q in range(count)], axis=dim)
    ordered = jnp.roll(by_offset, me, axis=dim)
    shape = block.shape
    return ordered.reshape(shape[:dim] + (count * shape[dim],) + shape[dim + 1 :])


def reduce_rows(block, dim):
    count = lax.axis_size("tile")
    shape = block.shape
    parts = block.reshape(shape[:dim] + (count, shape[dim] // count) + shape[dim + 1 :])
    received = lax.all_to_all(parts, "tile", dim, dim, tiled=True)
    return jnp.sum(received, axis=dim)


def body(
    perturbations, innovations, obs_weight, obs_cell, row_start, row_length, lat_rate, lon_rate
):
    slots = perturbations.shape[1]
    lat_rows = perturbations.shape[2]
    levels = perturbations.shape[3]
    nlon = perturbations.shape[4]
    groups = lax.axis_size("mem")
    own_levels = levels // groups
    shard_cols = own_levels * nlon
    first = lax.axis_index("mem") * own_levels
    lat_own = lax.dynamic_slice_in_dim(lat_rate, first, own_levels)
    lon_own = lax.dynamic_slice_in_dim(lon_rate, first, own_levels)

    tiles = lax.axis_size("tile")
    local_members = perturbations.shape[0]
    share = local_members // tiles
    if share and local_members % tiles == 0:
        sent = perturbations.astype(jnp.float32).reshape(
            tiles, share, slots, lat_rows, groups, own_levels, nlon
        )
        sent = sent.transpose(0, 4, 2, 5, 3, 1, 6).reshape(
            tiles * groups, slots, own_levels, lat_rows, share, nlon
        )
        got = lax.all_to_all(sent, ("tile", "mem"), 0, 0, tiled=True)
        pert = got.reshape(tiles, groups, slots, own_levels, lat_rows, share, nlon)
        pert = pert.transpose(2, 3, 0, 4, 1, 5, 6).reshape(
            slots, own_levels, tiles * lat_rows, groups * share, nlon
        )
    else:
        pert = lax.all_to_all(
            perturbations.astype(jnp.float32).transpose(1, 3, 2, 0, 4),
            "mem",
            split_axis=1,
            concat_axis=3,
            tiled=True,
        )
        pert = lax.all_to_all(pert, "tile", split_axis=3, concat_axis=2, tiled=True)

    def smooth(field):
        current = mask * field
        for inner in range(STEPS):
            current = diffuse_step(current, mask, lat_own, lon_own)
        return current

    def forward(control):
        smoothed = smooth(control)
        return reduce_rows(jnp.sum(pert * smoothed[None], axis=3), 2)

    def adjoint(gradient):
        return smooth(jnp.sum(pert * gradient[:, :, :, None], axis=0))

    def to_output(control):
        if share and local_members % tiles == 0:
            sent = control.reshape(own_levels, tiles, lat_rows, groups, share, nlon)
            sent = sent.transpose(1, 3, 0, 2, 4, 5).reshape(
                tiles * groups, own_levels, lat_rows, share, nlon
            )
            got = lax.all_to_all(sent, ("tile", "mem"), 0, 0, tiled=True)
            control = got.reshape(tiles, groups, own_levels, lat_rows, share, nlon)
            control = control.transpose(0, 4, 3, 1, 2, 5).reshape(
                tiles * share, lat_rows, levels, nlon
            )
        else:
            control = lax.all_to_all(control, "tile", split_axis=1, concat_axis=2, tiled=True)
            control = lax.all_to_all(control, "mem", split_axis=2, concat_axis=0, tiled=True)
            control = control.transpose(2, 1, 0, 3)
        return control

    local_cells = obs_cell[0]
    innov = innovations[0]
    weight = obs_weight[0]
    size = slots * lat_rows * shard_cols
    state_shape = (slots, own_levels, lat_rows, nlon)
    gathered = add_at_cells(local_cells, jnp.stack([weight * innov, weight], axis=1), size)
    gathered = gathered.reshape(slots, lat_rows, own_levels, nlon, 2).transpose(4, 0, 2, 1, 3)
    obs_diag = gathered[1]

    tables = jnp.zeros((lat_rows, nlon), jnp.float32)
    tables = tables.at[:, 0].set(row_start.astype(jnp.float32))
    tables = tables.at[:, 1].set(row_length.astype(jnp.float32))
    payload = jnp.concatenate(
        [gathered[0].reshape(slots * own_levels, lat_rows, nlon), tables[None]], axis=0
    )
    payload = gather_rows_by_permutes(payload, 1)
    tables = payload[-1, :, :2].astype(jnp.int32)
    mask = row_mask(tables[:, 0], tables[:, 1], nlon)
    first_grad = payload[:-1].reshape(slots, own_levels, tiles * lat_rows, nlon)

    residual = adjoint(first_grad)
    direction = residual
    control = jnp.zeros_like(residual)
    increment = jnp.zeros(state_shape, jnp.float32)
    norm_now = None
    for step in range(ITERS):
        state = forward(direction)
        image = direction + adjoint(gather_rows(obs_diag * state, 2))
        if norm_now is None:
            sums = global_sum(jnp.stack([jnp.sum(residual * residual), jnp.sum(direction * image)]))
            norm_now, curvature = sums[0], sums[1]
        else:
            curvature = global_sum(jnp.sum(direction * image))
        alpha = norm_now / curvature
        control = control + alpha * direction
        increment = increment + alpha * state
        if step + 1 < ITERS:
            residual = residual - alpha * image
            norm_next = global_sum(jnp.sum(residual * residual))
            direction = residual + norm_next / norm_now * direction
            norm_now = norm_next
    control = to_output(control)
    increment = increment.transpose(0, 2, 1, 3).reshape(slots, lat_rows, shard_cols)
    return (control, increment)


def solution(mesh):
    return jax.shard_map(
        body,
        mesh=mesh,
        in_specs=(
            P("mem", None, "tile", None, None),
            P("tile", "mem"),
            P("tile", "mem"),
            P("tile", "mem"),
            P("tile"),
            P("tile"),
            P(),
            P(),
        ),
        out_specs=(P("mem", "tile", None, None), P(None, "tile", "mem")),
        check_vma=False,
    )
```

```python
import jax
import jax.numpy as jnp
from jax import lax
from jax.sharding import PartitionSpec as P

ITERS = 2
STEPS = 8


def row_mask(starts, lengths, nlon):
    lon = lax.broadcasted_iota(jnp.int32, (starts.shape[0], nlon), 1)
    rel = (lon - starts[:, None]) % nlon
    return jnp.where(rel < lengths[:, None], 1.0, 0.0).astype(jnp.float32)[:, None, :]


def diffuse_step(field, mask, lat_rate, lon_rate):
    zero = jnp.zeros_like(field[:, :1])
    north = jnp.concatenate([field[:, 1:], zero], axis=1)
    south = jnp.concatenate([zero, field[:, :-1]], axis=1)
    east = jnp.roll(field, -1, axis=3)
    west = jnp.roll(field, 1, axis=3)
    lat_term = north + south - 2.0 * field
    lon_term = east + west - 2.0 * field
    return mask * (
        field + lat_rate[:, None, None, None] * lat_term + lon_rate[:, None, None, None] * lon_term
    )


def global_sum(value):
    axes = ("tile", "mem")
    count = lax.axis_size(axes)
    value = jnp.asarray(value, jnp.float32)
    spread = jnp.broadcast_to(value, (count,) + value.shape)
    return jnp.sum(lax.all_to_all(spread, axes, 0, 0, tiled=True), axis=0)


def add_at_cells(cells, values, size):
    lanes = 128
    count, kinds = values.shape
    high = lax.broadcasted_iota(jnp.int32, (count, size // lanes), 1) == (cells // lanes)[:, None]
    low = lax.broadcasted_iota(jnp.int32, (count, lanes), 1) == (cells % lanes)[:, None]
    spread = values[:, :, None] * low.astype(jnp.float32)[:, None, :]
    summed = jnp.dot(
        high.astype(jnp.float32).T,
        spread.reshape(count, kinds * lanes),
        precision=lax.Precision.HIGHEST,
        preferred_element_type=jnp.float32,
    )
    return summed.reshape(size // lanes, kinds, lanes).transpose(0, 2, 1).reshape(size, kinds)


def gather_rows(block, dim):
    count = lax.axis_size("tile")
    shape = block.shape
    copies = jnp.broadcast_to(
        jnp.expand_dims(block, dim), shape[:dim] + (count,) + shape[dim:]
    )
    joined = lax.all_to_all(copies, "tile", dim, dim, tiled=True)
    return joined.reshape(shape[:dim] + (count * shape[dim],) + shape[dim + 1 :])


def gather_rows_by_permutes(block, dim):
    count = lax.axis_size("tile")
    me = lax.axis_index("tile")
    pieces = [block] + [
        lax.ppermute(block, "tile", [(i, (i + k) % count) for i in range(count)])
        for k in range(1, count)
    ]
    by_offset = jnp.stack([pieces[(count - q) % count] for q in range(count)], axis=dim)
    ordered = jnp.roll(by_offset, me, axis=dim)
    shape = block.shape
    return ordered.reshape(shape[:dim] + (count * shape[dim],) + shape[dim + 1 :])


def reduce_rows_by_permutes(block, dim):
    count = lax.axis_size("tile")
    me = lax.axis_index("tile")
    share = block.shape[dim] // count
    total = lax.dynamic_slice_in_dim(block, me * share, share, axis=dim)
    for k in range(1, count):
        piece = lax.dynamic_slice_in_dim(block, ((me + k) % count) * share, share, axis=dim)
        total = total + lax.ppermute(piece, "tile", [(i, (i + k) % count) for i in range(count)])
    return total


def reduce_rows(block, dim):
    count = lax.axis_size("tile")
    shape = block.shape
    parts = block.reshape(shape[:dim] + (count, shape[dim] // count) + shape[dim + 1 :])
    received = lax.all_to_all(parts, "tile", dim, dim, tiled=True)
    return jnp.sum(received, axis=dim)


def body(
    perturbations, innovations, obs_weight, obs_cell, row_start, row_length, lat_rate, lon_rate
):
    slots = perturbations.shape[1]
    lat_rows = perturbations.shape[2]
    levels = perturbations.shape[3]
    nlon = perturbations.shape[4]
    groups = lax.axis_size("mem")
    own_levels = levels // groups
    shard_cols = own_levels * nlon
    first = lax.axis_index("mem") * own_levels
    lat_own = lax.dynamic_slice_in_dim(lat_rate, first, own_levels)
    lon_own = lax.dynamic_slice_in_dim(lon_rate, first, own_levels)

    tiles = lax.axis_size("tile")
    local_members = perturbations.shape[0]
    share = local_members // tiles
    if share and local_members % tiles == 0:
        sent = perturbations.astype(jnp.float32).reshape(
            tiles, share, slots, lat_rows, groups, own_levels, nlon
        )
        sent = sent.transpose(0, 4, 2, 5, 3, 1, 6).reshape(
            tiles * groups, slots, own_levels, lat_rows, share, nlon
        )
        got = lax.all_to_all(sent, ("tile", "mem"), 0, 0, tiled=True)
        pert = got.reshape(tiles, groups, slots, own_levels, lat_rows, share, nlon)
        pert = pert.transpose(2, 3, 0, 4, 1, 5, 6).reshape(
            slots, own_levels, tiles * lat_rows, groups * share, nlon
        )
    else:
        pert = lax.all_to_all(
            perturbations.astype(jnp.float32).transpose(1, 3, 2, 0, 4),
            "mem",
            split_axis=1,
            concat_axis=3,
            tiled=True,
        )
        pert = lax.all_to_all(pert, "tile", split_axis=3, concat_axis=2, tiled=True)

    def smooth(field):
        current = mask * field
        for inner in range(STEPS):
            current = diffuse_step(current, mask, lat_own, lon_own)
        return current

    def forward(control):
        smoothed = smooth(control)
        return reduce_rows_by_permutes(jnp.sum(pert * smoothed[None], axis=3), 2)

    def adjoint(gradient):
        return smooth(jnp.sum(pert * gradient[:, :, :, None], axis=0))

    def to_output(control):
        if share and local_members % tiles == 0:
            sent = control.reshape(own_levels, tiles, lat_rows, groups, share, nlon)
            sent = sent.transpose(1, 3, 0, 2, 4, 5).reshape(
                tiles * groups, own_levels, lat_rows, share, nlon
            )
            got = lax.all_to_all(sent, ("tile", "mem"), 0, 0, tiled=True)
            control = got.reshape(tiles, groups, own_levels, lat_rows, share, nlon)
            control = control.transpose(0, 4, 3, 1, 2, 5).reshape(
                tiles * share, lat_rows, levels, nlon
            )
        else:
            control = lax.all_to_all(control, "tile", split_axis=1, concat_axis=2, tiled=True)
            control = lax.all_to_all(control, "mem", split_axis=2, concat_axis=0, tiled=True)
            control = control.transpose(2, 1, 0, 3)
        return control

    local_cells = obs_cell[0]
    innov = innovations[0]
    weight = obs_weight[0]
    size = slots * lat_rows * shard_cols
    state_shape = (slots, own_levels, lat_rows, nlon)
    gathered = add_at_cells(local_cells, jnp.stack([weight * innov, weight], axis=1), size)
    gathered = gathered.reshape(slots, lat_rows, own_levels, nlon, 2).transpose(4, 0, 2, 1, 3)
    obs_diag = gathered[1]

    tables = jnp.zeros((lat_rows, nlon), jnp.float32)
    tables = tables.at[:, 0].set(row_start.astype(jnp.float32))
    tables = tables.at[:, 1].set(row_length.astype(jnp.float32))
    payload = jnp.concatenate(
        [gathered[0].reshape(slots * own_levels, lat_rows, nlon), tables[None]], axis=0
    )
    payload = gather_rows_by_permutes(payload, 1)
    tables = payload[-1, :, :2].astype(jnp.int32)
    mask = row_mask(tables[:, 0], tables[:, 1], nlon)
    first_grad = payload[:-1].reshape(slots, own_levels, tiles * lat_rows, nlon)

    residual = adjoint(first_grad)
    direction = residual
    control = jnp.zeros_like(residual)
    increment = jnp.zeros(state_shape, jnp.float32)
    norm_now = None
    for step in range(ITERS):
        state = forward(direction)
        image = direction + adjoint(gather_rows_by_permutes(obs_diag * state, 2))
        if norm_now is None:
            sums = global_sum(jnp.stack([jnp.sum(residual * residual), jnp.sum(direction * image)]))
            norm_now, curvature = sums[0], sums[1]
        else:
            curvature = global_sum(jnp.sum(direction * image))
        alpha = norm_now / curvature
        control = control + alpha * direction
        increment = increment + alpha * state
        if step + 1 < ITERS:
            residual = residual - alpha * image
            norm_next = global_sum(jnp.sum(residual * residual))
            direction = residual + norm_next / norm_now * direction
            norm_now = norm_next
    control = to_output(control)
    increment = increment.transpose(0, 2, 1, 3).reshape(slots, lat_rows, shard_cols)
    return (control, increment)


def solution(mesh):
    return jax.shard_map(
        body,
        mesh=mesh,
        in_specs=(
            P("mem", None, "tile", None, None),
            P("tile", "mem"),
            P("tile", "mem"),
            P("tile", "mem"),
            P("tile"),
            P("tile"),
            P(),
            P(),
        ),
        out_specs=(P("mem", "tile", None, None), P(None, "tile", "mem")),
        check_vma=False,
    )
```

```python
import jax
import jax.numpy as jnp
from jax import lax
from jax.sharding import PartitionSpec as P

ITERS = 2
STEPS = 8


def row_mask(starts, lengths, nlon):
    lon = lax.broadcasted_iota(jnp.int32, (starts.shape[0], nlon), 1)
    rel = (lon - starts[:, None]) % nlon
    return jnp.where(rel < lengths[:, None], 1.0, 0.0).astype(jnp.float32)[:, None, :]


def diffuse_step(field, mask, lat_rate, lon_rate):
    zero = jnp.zeros_like(field[:, :1])
    north = jnp.concatenate([field[:, 1:], zero], axis=1)
    south = jnp.concatenate([zero, field[:, :-1]], axis=1)
    east = jnp.roll(field, -1, axis=3)
    west = jnp.roll(field, 1, axis=3)
    lat_term = north + south - 2.0 * field
    lon_term = east + west - 2.0 * field
    return mask * (
        field + lat_rate[:, None, None, None] * lat_term + lon_rate[:, None, None, None] * lon_term
    )


def global_sum(value):
    axes = ("tile", "mem")
    count = lax.axis_size(axes)
    value = jnp.asarray(value, jnp.float32)
    spread = jnp.broadcast_to(value, (count,) + value.shape)
    return jnp.sum(lax.all_to_all(spread, axes, 0, 0, tiled=True), axis=0)


def add_at_cells(cells, values, size):
    lanes = 128
    count, kinds = values.shape
    high = lax.broadcasted_iota(jnp.int32, (count, size // lanes), 1) == (cells // lanes)[:, None]
    low = lax.broadcasted_iota(jnp.int32, (count, lanes), 1) == (cells % lanes)[:, None]
    spread = values[:, :, None] * low.astype(jnp.float32)[:, None, :]
    summed = jnp.dot(
        high.astype(jnp.float32).T,
        spread.reshape(count, kinds * lanes),
        precision=lax.Precision.HIGHEST,
        preferred_element_type=jnp.float32,
    )
    return summed.reshape(size // lanes, kinds, lanes).transpose(0, 2, 1).reshape(size, kinds)


def gather_rows(block, dim):
    count = lax.axis_size("tile")
    shape = block.shape
    copies = jnp.broadcast_to(
        jnp.expand_dims(block, dim), shape[:dim] + (count,) + shape[dim:]
    )
    joined = lax.all_to_all(copies, "tile", dim, dim, tiled=True)
    return joined.reshape(shape[:dim] + (count * shape[dim],) + shape[dim + 1 :])


def gather_rows_by_permutes(block, dim):
    count = lax.axis_size("tile")
    me = lax.axis_index("tile")
    pieces = [block] + [
        lax.ppermute(block, "tile", [(i, (i + k) % count) for i in range(count)])
        for k in range(1, count)
    ]
    by_offset = jnp.stack([pieces[(count - q) % count] for q in range(count)], axis=dim)
    ordered = jnp.roll(by_offset, me, axis=dim)
    shape = block.shape
    return ordered.reshape(shape[:dim] + (count * shape[dim],) + shape[dim + 1 :])


def reduce_rows_by_permutes(block, dim):
    count = lax.axis_size("tile")
    me = lax.axis_index("tile")
    share = block.shape[dim] // count
    total = lax.dynamic_slice_in_dim(block, me * share, share, axis=dim)
    for k in range(1, count):
        piece = lax.dynamic_slice_in_dim(block, ((me + k) % count) * share, share, axis=dim)
        total = total + lax.ppermute(piece, "tile", [(i, (i + k) % count) for i in range(count)])
    return total


def sum_over_tile_by_permutes(block):
    count = lax.axis_size("tile")
    total = block
    for k in range(1, count):
        total = total + lax.ppermute(block, "tile", [(i, (i + k) % count) for i in range(count)])
    return total


def reduce_rows(block, dim):
    count = lax.axis_size("tile")
    shape = block.shape
    parts = block.reshape(shape[:dim] + (count, shape[dim] // count) + shape[dim + 1 :])
    received = lax.all_to_all(parts, "tile", dim, dim, tiled=True)
    return jnp.sum(received, axis=dim)


def body(
    perturbations, innovations, obs_weight, obs_cell, row_start, row_length, lat_rate, lon_rate
):
    slots = perturbations.shape[1]
    lat_rows = perturbations.shape[2]
    levels = perturbations.shape[3]
    nlon = perturbations.shape[4]
    groups = lax.axis_size("mem")
    own_levels = levels // groups
    shard_cols = own_levels * nlon
    first = lax.axis_index("mem") * own_levels
    lat_own = lax.dynamic_slice_in_dim(lat_rate, first, own_levels)
    lon_own = lax.dynamic_slice_in_dim(lon_rate, first, own_levels)

    tiles = lax.axis_size("tile")
    local_members = perturbations.shape[0]
    share = local_members // tiles
    if share and local_members % tiles == 0:
        sent = perturbations.astype(jnp.float32).reshape(
            tiles, share, slots, lat_rows, groups, own_levels, nlon
        )
        sent = sent.transpose(0, 4, 2, 5, 3, 1, 6).reshape(
            tiles * groups, slots, own_levels, lat_rows, share, nlon
        )
        got = lax.all_to_all(sent, ("tile", "mem"), 0, 0, tiled=True)
        pert = got.reshape(tiles, groups, slots, own_levels, lat_rows, share, nlon)
        pert = pert.transpose(2, 3, 0, 4, 1, 5, 6).reshape(
            slots, own_levels, tiles * lat_rows, groups * share, nlon
        )
    else:
        pert = lax.all_to_all(
            perturbations.astype(jnp.float32).transpose(1, 3, 2, 0, 4),
            "mem",
            split_axis=1,
            concat_axis=3,
            tiled=True,
        )
        pert = lax.all_to_all(pert, "tile", split_axis=3, concat_axis=2, tiled=True)

    def smooth(field):
        current = mask * field
        for inner in range(STEPS):
            current = diffuse_step(current, mask, lat_own, lon_own)
        return current

    def forward(control):
        smoothed = smooth(control)
        return sum_over_tile_by_permutes(jnp.sum(pert * smoothed[None], axis=3))

    def adjoint(gradient):
        return smooth(jnp.sum(pert * gradient[:, :, :, None], axis=0))

    def to_output(control):
        if share and local_members % tiles == 0:
            sent = control.reshape(own_levels, tiles, lat_rows, groups, share, nlon)
            sent = sent.transpose(1, 3, 0, 2, 4, 5).reshape(
                tiles * groups, own_levels, lat_rows, share, nlon
            )
            got = lax.all_to_all(sent, ("tile", "mem"), 0, 0, tiled=True)
            control = got.reshape(tiles, groups, own_levels, lat_rows, share, nlon)
            control = control.transpose(0, 4, 3, 1, 2, 5).reshape(
                tiles * share, lat_rows, levels, nlon
            )
        else:
            control = lax.all_to_all(control, "tile", split_axis=1, concat_axis=2, tiled=True)
            control = lax.all_to_all(control, "mem", split_axis=2, concat_axis=0, tiled=True)
            control = control.transpose(2, 1, 0, 3)
        return control

    local_cells = obs_cell[0]
    innov = innovations[0]
    weight = obs_weight[0]
    size = slots * lat_rows * shard_cols
    state_shape = (slots, own_levels, lat_rows, nlon)
    gathered = add_at_cells(local_cells, jnp.stack([weight * innov, weight], axis=1), size)
    gathered = gathered.reshape(slots, lat_rows, own_levels, nlon, 2).transpose(4, 0, 2, 1, 3)

    tables = jnp.zeros((lat_rows, nlon), jnp.float32)
    tables = tables.at[:, 0].set(row_start.astype(jnp.float32))
    tables = tables.at[:, 1].set(row_length.astype(jnp.float32))
    payload = jnp.concatenate(
        [gathered.reshape(2 * slots * own_levels, lat_rows, nlon), tables[None]], axis=0
    )
    payload = gather_rows_by_permutes(payload, 1)
    tables = payload[-1, :, :2].astype(jnp.int32)
    mask = row_mask(tables[:, 0], tables[:, 1], nlon)
    both = payload[:-1].reshape(2, slots, own_levels, tiles * lat_rows, nlon)
    first_grad, obs_diag = both[0], both[1]
    me = lax.axis_index("tile")

    residual = adjoint(first_grad)
    direction = residual
    control = jnp.zeros_like(residual)
    increment = jnp.zeros(state_shape, jnp.float32)
    norm_now = None
    for step in range(ITERS):
        state = forward(direction)
        image = direction + adjoint(obs_diag * state)
        if norm_now is None:
            sums = global_sum(jnp.stack([jnp.sum(residual * residual), jnp.sum(direction * image)]))
            norm_now, curvature = sums[0], sums[1]
        else:
            curvature = global_sum(jnp.sum(direction * image))
        alpha = norm_now / curvature
        control = control + alpha * direction
        own_state = lax.dynamic_slice_in_dim(state, me * lat_rows, lat_rows, axis=2)
        increment = increment + alpha * own_state
        if step + 1 < ITERS:
            residual = residual - alpha * image
            norm_next = global_sum(jnp.sum(residual * residual))
            direction = residual + norm_next / norm_now * direction
            norm_now = norm_next
    control = to_output(control)
    increment = increment.transpose(0, 2, 1, 3).reshape(slots, lat_rows, shard_cols)
    return (control, increment)


def solution(mesh):
    return jax.shard_map(
        body,
        mesh=mesh,
        in_specs=(
            P("mem", None, "tile", None, None),
            P("tile", "mem"),
            P("tile", "mem"),
            P("tile", "mem"),
            P("tile"),
            P("tile"),
            P(),
            P(),
        ),
        out_specs=(P("mem", "tile", None, None), P(None, "tile", "mem")),
        check_vma=False,
    )
```

```python
import jax
import jax.numpy as jnp
from jax import lax
from jax.sharding import PartitionSpec as P

ITERS = 2
STEPS = 8


def row_mask(starts, lengths, nlon):
    lon = lax.broadcasted_iota(jnp.int32, (starts.shape[0], nlon), 1)
    rel = (lon - starts[:, None]) % nlon
    return jnp.where(rel < lengths[:, None], 1.0, 0.0).astype(jnp.float32)[:, None, :]


def diffuse_step(field, mask, lat_rate, lon_rate):
    zero = jnp.zeros_like(field[:, :1])
    north = jnp.concatenate([field[:, 1:], zero], axis=1)
    south = jnp.concatenate([zero, field[:, :-1]], axis=1)
    east = jnp.roll(field, -1, axis=3)
    west = jnp.roll(field, 1, axis=3)
    lat_term = north + south - 2.0 * field
    lon_term = east + west - 2.0 * field
    return mask * (
        field + lat_rate[:, None, None, None] * lat_term + lon_rate[:, None, None, None] * lon_term
    )


def global_sum(value):
    axes = ("tile", "mem")
    count = lax.axis_size(axes)
    value = jnp.asarray(value, jnp.float32)
    spread = jnp.broadcast_to(value, (count,) + value.shape)
    return jnp.sum(lax.all_to_all(spread, axes, 0, 0, tiled=True), axis=0)


def add_at_cells(cells, values, size):
    lanes = 128
    count, kinds = values.shape
    high = lax.broadcasted_iota(jnp.int32, (count, size // lanes), 1) == (cells // lanes)[:, None]
    low = lax.broadcasted_iota(jnp.int32, (count, lanes), 1) == (cells % lanes)[:, None]
    spread = values[:, :, None] * low.astype(jnp.float32)[:, None, :]
    summed = jnp.dot(
        high.astype(jnp.float32).T,
        spread.reshape(count, kinds * lanes),
        precision=lax.Precision.HIGHEST,
        preferred_element_type=jnp.float32,
    )
    return summed.reshape(size // lanes, kinds, lanes).transpose(0, 2, 1).reshape(size, kinds)


def gather_rows(block, dim):
    count = lax.axis_size("tile")
    shape = block.shape
    copies = jnp.broadcast_to(
        jnp.expand_dims(block, dim), shape[:dim] + (count,) + shape[dim:]
    )
    joined = lax.all_to_all(copies, "tile", dim, dim, tiled=True)
    return joined.reshape(shape[:dim] + (count * shape[dim],) + shape[dim + 1 :])


def gather_rows_by_permutes(block, dim):
    count = lax.axis_size("tile")
    me = lax.axis_index("tile")
    pieces = [block] + [
        lax.ppermute(block, "tile", [(i, (i + k) % count) for i in range(count)])
        for k in range(1, count)
    ]
    by_offset = jnp.stack([pieces[(count - q) % count] for q in range(count)], axis=dim)
    ordered = jnp.roll(by_offset, me, axis=dim)
    shape = block.shape
    return ordered.reshape(shape[:dim] + (count * shape[dim],) + shape[dim + 1 :])


def reduce_rows_by_permutes(block, dim):
    count = lax.axis_size("tile")
    me = lax.axis_index("tile")
    share = block.shape[dim] // count
    total = lax.dynamic_slice_in_dim(block, me * share, share, axis=dim)
    for k in range(1, count):
        piece = lax.dynamic_slice_in_dim(block, ((me + k) % count) * share, share, axis=dim)
        total = total + lax.ppermute(piece, "tile", [(i, (i + k) % count) for i in range(count)])
    return total


def sum_over_tile_by_permutes(block):
    count = lax.axis_size("tile")
    total = block
    for k in range(1, count):
        total = total + lax.ppermute(block, "tile", [(i, (i + k) % count) for i in range(count)])
    return total


def reduce_rows(block, dim):
    count = lax.axis_size("tile")
    shape = block.shape
    parts = block.reshape(shape[:dim] + (count, shape[dim] // count) + shape[dim + 1 :])
    received = lax.all_to_all(parts, "tile", dim, dim, tiled=True)
    return jnp.sum(received, axis=dim)


def body(
    perturbations, innovations, obs_weight, obs_cell, row_start, row_length, lat_rate, lon_rate
):
    slots = perturbations.shape[1]
    lat_rows = perturbations.shape[2]
    levels = perturbations.shape[3]
    nlon = perturbations.shape[4]
    groups = lax.axis_size("mem")
    own_levels = levels // groups
    shard_cols = own_levels * nlon
    first = lax.axis_index("mem") * own_levels
    lat_own = lax.dynamic_slice_in_dim(lat_rate, first, own_levels)
    lon_own = lax.dynamic_slice_in_dim(lon_rate, first, own_levels)

    tiles = lax.axis_size("tile")
    local_members = perturbations.shape[0]
    share = local_members // tiles
    if share and local_members % tiles == 0:
        sent = perturbations.astype(jnp.float32).reshape(
            tiles, share, slots, lat_rows, groups, own_levels, nlon
        )
        sent = sent.transpose(0, 4, 2, 5, 3, 1, 6).reshape(
            tiles * groups, slots, own_levels, lat_rows, share, nlon
        )
        got = lax.all_to_all(sent, ("tile", "mem"), 0, 0, tiled=True)
        pert = got.reshape(tiles, groups, slots, own_levels, lat_rows, share, nlon)
        pert = pert.transpose(2, 3, 0, 4, 1, 5, 6).reshape(
            slots, own_levels, tiles * lat_rows, groups * share, nlon
        )
    else:
        pert = lax.all_to_all(
            perturbations.astype(jnp.float32).transpose(1, 3, 2, 0, 4),
            "mem",
            split_axis=1,
            concat_axis=3,
            tiled=True,
        )
        pert = lax.all_to_all(pert, "tile", split_axis=3, concat_axis=2, tiled=True)

    def smooth(field):
        current = mask * field
        return lax.fori_loop(
            0, STEPS, lambda inner, now: diffuse_step(now, mask, lat_own, lon_own), current, unroll=4
        )

    def forward(control):
        smoothed = smooth(control)
        return sum_over_tile_by_permutes(jnp.sum(pert * smoothed[None], axis=3))

    def adjoint(gradient):
        return smooth(jnp.sum(pert * gradient[:, :, :, None], axis=0))

    def to_output(control):
        if share and local_members % tiles == 0:
            sent = control.reshape(own_levels, tiles, lat_rows, groups, share, nlon)
            sent = sent.transpose(1, 3, 0, 2, 4, 5).reshape(
                tiles * groups, own_levels, lat_rows, share, nlon
            )
            got = lax.all_to_all(sent, ("tile", "mem"), 0, 0, tiled=True)
            control = got.reshape(tiles, groups, own_levels, lat_rows, share, nlon)
            control = control.transpose(0, 4, 3, 1, 2, 5).reshape(
                tiles * share, lat_rows, levels, nlon
            )
        else:
            control = lax.all_to_all(control, "tile", split_axis=1, concat_axis=2, tiled=True)
            control = lax.all_to_all(control, "mem", split_axis=2, concat_axis=0, tiled=True)
            control = control.transpose(2, 1, 0, 3)
        return control

    local_cells = obs_cell[0]
    innov = innovations[0]
    weight = obs_weight[0]
    size = slots * lat_rows * shard_cols
    state_shape = (slots, own_levels, lat_rows, nlon)
    gathered = add_at_cells(local_cells, jnp.stack([weight * innov, weight], axis=1), size)
    gathered = gathered.reshape(slots, lat_rows, own_levels, nlon, 2).transpose(4, 0, 2, 1, 3)

    tables = jnp.zeros((lat_rows, nlon), jnp.float32)
    tables = tables.at[:, 0].set(row_start.astype(jnp.float32))
    tables = tables.at[:, 1].set(row_length.astype(jnp.float32))
    payload = jnp.concatenate(
        [gathered.reshape(2 * slots * own_levels, lat_rows, nlon), tables[None]], axis=0
    )
    payload = gather_rows_by_permutes(payload, 1)
    tables = payload[-1, :, :2].astype(jnp.int32)
    mask = row_mask(tables[:, 0], tables[:, 1], nlon)
    both = payload[:-1].reshape(2, slots, own_levels, tiles * lat_rows, nlon)
    first_grad, obs_diag = both[0], both[1]
    me = lax.axis_index("tile")

    residual = adjoint(first_grad)
    direction = residual
    control = jnp.zeros_like(residual)
    increment = jnp.zeros(state_shape, jnp.float32)
    norm_now = None
    for step in range(ITERS):
        state = forward(direction)
        image = direction + adjoint(obs_diag * state)
        if norm_now is None:
            sums = global_sum(jnp.stack([jnp.sum(residual * residual), jnp.sum(direction * image)]))
            norm_now, curvature = sums[0], sums[1]
        else:
            curvature = global_sum(jnp.sum(direction * image))
        alpha = norm_now / curvature
        control = control + alpha * direction
        own_state = lax.dynamic_slice_in_dim(state, me * lat_rows, lat_rows, axis=2)
        increment = increment + alpha * own_state
        if step + 1 < ITERS:
            residual = residual - alpha * image
            norm_next = global_sum(jnp.sum(residual * residual))
            direction = residual + norm_next / norm_now * direction
            norm_now = norm_next
    control = to_output(control)
    increment = increment.transpose(0, 2, 1, 3).reshape(slots, lat_rows, shard_cols)
    return (control, increment)


def solution(mesh):
    return jax.shard_map(
        body,
        mesh=mesh,
        in_specs=(
            P("mem", None, "tile", None, None),
            P("tile", "mem"),
            P("tile", "mem"),
            P("tile", "mem"),
            P("tile"),
            P("tile"),
            P(),
            P(),
        ),
        out_specs=(P("mem", "tile", None, None), P(None, "tile", "mem")),
        check_vma=False,
    )
```

```python
import jax
import jax.numpy as jnp
from jax import lax
from jax.experimental import pallas as pl
from jax.experimental.pallas import tpu as pltpu
from jax.sharding import PartitionSpec as P

ITERS = 2
STEPS = 8


def row_mask(starts, lengths, nlon):
    lon = lax.broadcasted_iota(jnp.int32, (starts.shape[0], nlon), 1)
    rel = (lon - starts[:, None]) % nlon
    return jnp.where(rel < lengths[:, None], 1.0, 0.0).astype(jnp.float32)[:, None, :]


def diffuse_step(field, mask, lat_rate, lon_rate):
    zero = jnp.zeros_like(field[:, :1])
    north = jnp.concatenate([field[:, 1:], zero], axis=1)
    south = jnp.concatenate([zero, field[:, :-1]], axis=1)
    east = jnp.roll(field, -1, axis=3)
    west = jnp.roll(field, 1, axis=3)
    lat_term = north + south - 2.0 * field
    lon_term = east + west - 2.0 * field
    return mask * (
        field + lat_rate[:, None, None, None] * lat_term + lon_rate[:, None, None, None] * lon_term
    )


def smooth_kernel(rates_ref, mask_ref, field_ref, out_ref):
    levels, rows, members, nlon = field_ref.shape
    mask = mask_ref[...]
    zero = jnp.zeros((1, members, nlon), jnp.float32)
    for level in range(levels):
        lat = rates_ref[0, level]
        lon = rates_ref[1, level]
        now = mask * field_ref[level]
        for inner in range(STEPS):
            north = jnp.concatenate([now[1:], zero], axis=0)
            south = jnp.concatenate([zero, now[:-1]], axis=0)
            east = pltpu.roll(now, nlon - 1, 2)
            west = pltpu.roll(now, 1, 2)
            lat_term = north + south - 2.0 * now
            lon_term = east + west - 2.0 * now
            now = mask * (now + lat * lat_term + lon * lon_term)
        out_ref[level] = now


def smooth_in_vmem(field, mask, lat_rate, lon_rate):
    size = field.size
    return pl.pallas_call(
        smooth_kernel,
        out_shape=jax.ShapeDtypeStruct(field.shape, jnp.float32),
        in_specs=[
            pl.BlockSpec(memory_space=pltpu.SMEM),
            pl.BlockSpec(memory_space=pltpu.VMEM),
            pl.BlockSpec(memory_space=pltpu.VMEM),
        ],
        out_specs=pl.BlockSpec(memory_space=pltpu.VMEM),
        cost_estimate=pl.CostEstimate(
            flops=14 * STEPS * size, bytes_accessed=8 * size, transcendentals=0
        ),
    )(jnp.stack([lat_rate, lon_rate]), mask, field)


def global_sum(value):
    axes = ("tile", "mem")
    count = lax.axis_size(axes)
    value = jnp.asarray(value, jnp.float32)
    spread = jnp.broadcast_to(value, (count,) + value.shape)
    return jnp.sum(lax.all_to_all(spread, axes, 0, 0, tiled=True), axis=0)


def add_at_cells(cells, values, size):
    lanes = 128
    count, kinds = values.shape
    high = lax.broadcasted_iota(jnp.int32, (count, size // lanes), 1) == (cells // lanes)[:, None]
    low = lax.broadcasted_iota(jnp.int32, (count, lanes), 1) == (cells % lanes)[:, None]
    spread = values[:, :, None] * low.astype(jnp.float32)[:, None, :]
    summed = jnp.dot(
        high.astype(jnp.float32).T,
        spread.reshape(count, kinds * lanes),
        precision=lax.Precision.HIGHEST,
        preferred_element_type=jnp.float32,
    )
    return summed.reshape(size // lanes, kinds, lanes).transpose(0, 2, 1).reshape(size, kinds)


def gather_rows(block, dim):
    count = lax.axis_size("tile")
    shape = block.shape
    copies = jnp.broadcast_to(
        jnp.expand_dims(block, dim), shape[:dim] + (count,) + shape[dim:]
    )
    joined = lax.all_to_all(copies, "tile", dim, dim, tiled=True)
    return joined.reshape(shape[:dim] + (count * shape[dim],) + shape[dim + 1 :])


def gather_rows_by_permutes(block, dim):
    count = lax.axis_size("tile")
    me = lax.axis_index("tile")
    pieces = [block] + [
        lax.ppermute(block, "tile", [(i, (i + k) % count) for i in range(count)])
        for k in range(1, count)
    ]
    by_offset = jnp.stack([pieces[(count - q) % count] for q in range(count)], axis=dim)
    ordered = jnp.roll(by_offset, me, axis=dim)
    shape = block.shape
    return ordered.reshape(shape[:dim] + (count * shape[dim],) + shape[dim + 1 :])


def reduce_rows_by_permutes(block, dim):
    count = lax.axis_size("tile")
    me = lax.axis_index("tile")
    share = block.shape[dim] // count
    total = lax.dynamic_slice_in_dim(block, me * share, share, axis=dim)
    for k in range(1, count):
        piece = lax.dynamic_slice_in_dim(block, ((me + k) % count) * share, share, axis=dim)
        total = total + lax.ppermute(piece, "tile", [(i, (i + k) % count) for i in range(count)])
    return total


def sum_over_tile_by_permutes(block):
    count = lax.axis_size("tile")
    total = block
    for k in range(1, count):
        total = total + lax.ppermute(block, "tile", [(i, (i + k) % count) for i in range(count)])
    return total


def reduce_rows(block, dim):
    count = lax.axis_size("tile")
    shape = block.shape
    parts = block.reshape(shape[:dim] + (count, shape[dim] // count) + shape[dim + 1 :])
    received = lax.all_to_all(parts, "tile", dim, dim, tiled=True)
    return jnp.sum(received, axis=dim)


def body(
    perturbations, innovations, obs_weight, obs_cell, row_start, row_length, lat_rate, lon_rate
):
    slots = perturbations.shape[1]
    lat_rows = perturbations.shape[2]
    levels = perturbations.shape[3]
    nlon = perturbations.shape[4]
    groups = lax.axis_size("mem")
    own_levels = levels // groups
    shard_cols = own_levels * nlon
    first = lax.axis_index("mem") * own_levels
    lat_own = lax.dynamic_slice_in_dim(lat_rate, first, own_levels)
    lon_own = lax.dynamic_slice_in_dim(lon_rate, first, own_levels)

    tiles = lax.axis_size("tile")
    local_members = perturbations.shape[0]
    share = local_members // tiles
    if share and local_members % tiles == 0:
        sent = perturbations.astype(jnp.float32).reshape(
            tiles, share, slots, lat_rows, groups, own_levels, nlon
        )
        sent = sent.transpose(0, 4, 2, 5, 3, 1, 6).reshape(
            tiles * groups, slots, own_levels, lat_rows, share, nlon
        )
        got = lax.all_to_all(sent, ("tile", "mem"), 0, 0, tiled=True)
        pert = got.reshape(tiles, groups, slots, own_levels, lat_rows, share, nlon)
        pert = pert.transpose(2, 3, 0, 4, 1, 5, 6).reshape(
            slots, own_levels, tiles * lat_rows, groups * share, nlon
        )
    else:
        pert = lax.all_to_all(
            perturbations.astype(jnp.float32).transpose(1, 3, 2, 0, 4),
            "mem",
            split_axis=1,
            concat_axis=3,
            tiled=True,
        )
        pert = lax.all_to_all(pert, "tile", split_axis=3, concat_axis=2, tiled=True)

    def smooth(field):
        return smooth_in_vmem(field, mask, lat_own, lon_own)

    def forward(control):
        smoothed = smooth(control)
        return sum_over_tile_by_permutes(jnp.sum(pert * smoothed[None], axis=3))

    def adjoint(gradient):
        return smooth(jnp.sum(pert * gradient[:, :, :, None], axis=0))

    def to_output(control):
        if share and local_members % tiles == 0:
            sent = control.reshape(own_levels, tiles, lat_rows, groups, share, nlon)
            sent = sent.transpose(1, 3, 0, 2, 4, 5).reshape(
                tiles * groups, own_levels, lat_rows, share, nlon
            )
            got = lax.all_to_all(sent, ("tile", "mem"), 0, 0, tiled=True)
            control = got.reshape(tiles, groups, own_levels, lat_rows, share, nlon)
            control = control.transpose(0, 4, 3, 1, 2, 5).reshape(
                tiles * share, lat_rows, levels, nlon
            )
        else:
            control = lax.all_to_all(control, "tile", split_axis=1, concat_axis=2, tiled=True)
            control = lax.all_to_all(control, "mem", split_axis=2, concat_axis=0, tiled=True)
            control = control.transpose(2, 1, 0, 3)
        return control

    local_cells = obs_cell[0]
    innov = innovations[0]
    weight = obs_weight[0]
    size = slots * lat_rows * shard_cols
    state_shape = (slots, own_levels, lat_rows, nlon)
    gathered = add_at_cells(local_cells, jnp.stack([weight * innov, weight], axis=1), size)
    gathered = gathered.reshape(slots, lat_rows, own_levels, nlon, 2).transpose(4, 0, 2, 1, 3)

    tables = jnp.zeros((lat_rows, nlon), jnp.float32)
    tables = tables.at[:, 0].set(row_start.astype(jnp.float32))
    tables = tables.at[:, 1].set(row_length.astype(jnp.float32))
    payload = jnp.concatenate(
        [gathered.reshape(2 * slots * own_levels, lat_rows, nlon), tables[None]], axis=0
    )
    payload = gather_rows_by_permutes(payload, 1)
    tables = payload[-1, :, :2].astype(jnp.int32)
    mask = row_mask(tables[:, 0], tables[:, 1], nlon)
    both = payload[:-1].reshape(2, slots, own_levels, tiles * lat_rows, nlon)
    first_grad, obs_diag = both[0], both[1]
    me = lax.axis_index("tile")

    residual = adjoint(first_grad)
    direction = residual
    control = jnp.zeros_like(residual)
    increment = jnp.zeros(state_shape, jnp.float32)
    norm_now = None
    for step in range(ITERS):
        state = forward(direction)
        image = direction + adjoint(obs_diag * state)
        if norm_now is None:
            sums = global_sum(jnp.stack([jnp.sum(residual * residual), jnp.sum(direction * image)]))
            norm_now, curvature = sums[0], sums[1]
        else:
            curvature = global_sum(jnp.sum(direction * image))
        alpha = norm_now / curvature
        control = control + alpha * direction
        own_state = lax.dynamic_slice_in_dim(state, me * lat_rows, lat_rows, axis=2)
        increment = increment + alpha * own_state
        if step + 1 < ITERS:
            residual = residual - alpha * image
            norm_next = global_sum(jnp.sum(residual * residual))
            direction = residual + norm_next / norm_now * direction
            norm_now = norm_next
    control = to_output(control)
    increment = increment.transpose(0, 2, 1, 3).reshape(slots, lat_rows, shard_cols)
    return (control, increment)


def solution(mesh):
    return jax.shard_map(
        body,
        mesh=mesh,
        in_specs=(
            P("mem", None, "tile", None, None),
            P("tile", "mem"),
            P("tile", "mem"),
            P("tile", "mem"),
            P("tile"),
            P("tile"),
            P(),
            P(),
        ),
        out_specs=(P("mem", "tile", None, None), P(None, "tile", "mem")),
        check_vma=False,
    )
```

```python
import jax
import jax.numpy as jnp
from jax import lax
from jax.experimental import pallas as pl
from jax.experimental.pallas import tpu as pltpu
from jax.sharding import PartitionSpec as P

ITERS = 2
STEPS = 8


def row_mask(starts, lengths, nlon):
    lon = lax.broadcasted_iota(jnp.int32, (starts.shape[0], nlon), 1)
    rel = (lon - starts[:, None]) % nlon
    return jnp.where(rel < lengths[:, None], 1.0, 0.0).astype(jnp.float32)[:, None, :]


def diffuse_step(field, mask, lat_rate, lon_rate):
    zero = jnp.zeros_like(field[:, :1])
    north = jnp.concatenate([field[:, 1:], zero], axis=1)
    south = jnp.concatenate([zero, field[:, :-1]], axis=1)
    east = jnp.roll(field, -1, axis=3)
    west = jnp.roll(field, 1, axis=3)
    lat_term = north + south - 2.0 * field
    lon_term = east + west - 2.0 * field
    return mask * (
        field + lat_rate[:, None, None, None] * lat_term + lon_rate[:, None, None, None] * lon_term
    )


def smooth_level(rates_ref, mask, now, level):
    rows, members, nlon = now.shape
    lat = rates_ref[0, level]
    lon = rates_ref[1, level]
    zero = jnp.zeros((1, members, nlon), jnp.float32)
    now = mask * now
    for inner in range(STEPS):
        north = jnp.concatenate([now[1:], zero], axis=0)
        south = jnp.concatenate([zero, now[:-1]], axis=0)
        east = pltpu.roll(now, nlon - 1, 2)
        west = pltpu.roll(now, 1, 2)
        lat_term = north + south - 2.0 * now
        lon_term = east + west - 2.0 * now
        now = mask * (now + lat * lat_term + lon * lon_term)
    return now


def adjoint_kernel(rates_ref, mask_ref, pert_ref, diag_ref, state_ref, out_ref):
    slots, levels = pert_ref.shape[:2]
    mask = mask_ref[...]
    for level in range(levels):
        field = None
        for slot in range(slots):
            grad = diag_ref[slot, level] * state_ref[slot, level]
            term = pert_ref[slot, level] * grad[:, None, :]
            field = term if field is None else field + term
        out_ref[level] = smooth_level(rates_ref, mask, field, level)


def forward_kernel(rates_ref, mask_ref, pert_ref, field_ref, out_ref):
    slots, levels = pert_ref.shape[:2]
    mask = mask_ref[...]
    for level in range(levels):
        smoothed = smooth_level(rates_ref, mask, field_ref[level], level)
        for slot in range(slots):
            out_ref[slot, level] = jnp.sum(pert_ref[slot, level] * smoothed, axis=1)


def local_call(kernel, out_shape, rates, *arrays):
    size = sum(a.size for a in arrays)
    return pl.pallas_call(
        kernel,
        out_shape=jax.ShapeDtypeStruct(out_shape, jnp.float32),
        in_specs=[pl.BlockSpec(memory_space=pltpu.SMEM)]
        + [pl.BlockSpec(memory_space=pltpu.VMEM)] * len(arrays),
        out_specs=pl.BlockSpec(memory_space=pltpu.VMEM),
        cost_estimate=pl.CostEstimate(
            flops=16 * STEPS * size, bytes_accessed=4 * size, transcendentals=0
        ),
    )(rates, *arrays)


def global_sum(value):
    axes = ("tile", "mem")
    count = lax.axis_size(axes)
    value = jnp.asarray(value, jnp.float32)
    spread = jnp.broadcast_to(value, (count,) + value.shape)
    return jnp.sum(lax.all_to_all(spread, axes, 0, 0, tiled=True), axis=0)


def add_at_cells(cells, values, size):
    lanes = 128
    count, kinds = values.shape
    high = lax.broadcasted_iota(jnp.int32, (count, size // lanes), 1) == (cells // lanes)[:, None]
    low = lax.broadcasted_iota(jnp.int32, (count, lanes), 1) == (cells % lanes)[:, None]
    spread = values[:, :, None] * low.astype(jnp.float32)[:, None, :]
    summed = jnp.dot(
        high.astype(jnp.float32).T,
        spread.reshape(count, kinds * lanes),
        precision=lax.Precision.HIGHEST,
        preferred_element_type=jnp.float32,
    )
    return summed.reshape(size // lanes, kinds, lanes).transpose(0, 2, 1).reshape(size, kinds)


def gather_rows(block, dim):
    count = lax.axis_size("tile")
    shape = block.shape
    copies = jnp.broadcast_to(
        jnp.expand_dims(block, dim), shape[:dim] + (count,) + shape[dim:]
    )
    joined = lax.all_to_all(copies, "tile", dim, dim, tiled=True)
    return joined.reshape(shape[:dim] + (count * shape[dim],) + shape[dim + 1 :])


def gather_rows_by_permutes(block, dim):
    count = lax.axis_size("tile")
    me = lax.axis_index("tile")
    pieces = [block] + [
        lax.ppermute(block, "tile", [(i, (i + k) % count) for i in range(count)])
        for k in range(1, count)
    ]
    by_offset = jnp.stack([pieces[(count - q) % count] for q in range(count)], axis=dim)
    ordered = jnp.roll(by_offset, me, axis=dim)
    shape = block.shape
    return ordered.reshape(shape[:dim] + (count * shape[dim],) + shape[dim + 1 :])


def reduce_rows_by_permutes(block, dim):
    count = lax.axis_size("tile")
    me = lax.axis_index("tile")
    share = block.shape[dim] // count
    total = lax.dynamic_slice_in_dim(block, me * share, share, axis=dim)
    for k in range(1, count):
        piece = lax.dynamic_slice_in_dim(block, ((me + k) % count) * share, share, axis=dim)
        total = total + lax.ppermute(piece, "tile", [(i, (i + k) % count) for i in range(count)])
    return total


def sum_over_tile_by_permutes(block):
    count = lax.axis_size("tile")
    total = block
    for k in range(1, count):
        total = total + lax.ppermute(block, "tile", [(i, (i + k) % count) for i in range(count)])
    return total


def reduce_rows(block, dim):
    count = lax.axis_size("tile")
    shape = block.shape
    parts = block.reshape(shape[:dim] + (count, shape[dim] // count) + shape[dim + 1 :])
    received = lax.all_to_all(parts, "tile", dim, dim, tiled=True)
    return jnp.sum(received, axis=dim)


def body(
    perturbations, innovations, obs_weight, obs_cell, row_start, row_length, lat_rate, lon_rate
):
    slots = perturbations.shape[1]
    lat_rows = perturbations.shape[2]
    levels = perturbations.shape[3]
    nlon = perturbations.shape[4]
    groups = lax.axis_size("mem")
    own_levels = levels // groups
    shard_cols = own_levels * nlon
    first = lax.axis_index("mem") * own_levels
    lat_own = lax.dynamic_slice_in_dim(lat_rate, first, own_levels)
    lon_own = lax.dynamic_slice_in_dim(lon_rate, first, own_levels)

    tiles = lax.axis_size("tile")
    local_members = perturbations.shape[0]
    share = local_members // tiles
    if share and local_members % tiles == 0:
        sent = perturbations.astype(jnp.float32).reshape(
            tiles, share, slots, lat_rows, groups, own_levels, nlon
        )
        sent = sent.transpose(0, 4, 2, 5, 3, 1, 6).reshape(
            tiles * groups, slots, own_levels, lat_rows, share, nlon
        )
        got = lax.all_to_all(sent, ("tile", "mem"), 0, 0, tiled=True)
        pert = got.reshape(tiles, groups, slots, own_levels, lat_rows, share, nlon)
        pert = pert.transpose(2, 3, 0, 4, 1, 5, 6).reshape(
            slots, own_levels, tiles * lat_rows, groups * share, nlon
        )
    else:
        pert = lax.all_to_all(
            perturbations.astype(jnp.float32).transpose(1, 3, 2, 0, 4),
            "mem",
            split_axis=1,
            concat_axis=3,
            tiled=True,
        )
        pert = lax.all_to_all(pert, "tile", split_axis=3, concat_axis=2, tiled=True)

    rates = jnp.stack([lat_own, lon_own])

    def forward(control):
        partial = local_call(
            forward_kernel,
            (slots, own_levels, control.shape[1], nlon),
            rates,
            mask,
            pert,
            control,
        )
        return sum_over_tile_by_permutes(partial)

    def adjoint(diag, state):
        return local_call(
            adjoint_kernel, pert.shape[1:], rates, mask, pert, diag, state
        )

    def to_output(control):
        if share and local_members % tiles == 0:
            sent = control.reshape(own_levels, tiles, lat_rows, groups, share, nlon)
            sent = sent.transpose(1, 3, 0, 2, 4, 5).reshape(
                tiles * groups, own_levels, lat_rows, share, nlon
            )
            got = lax.all_to_all(sent, ("tile", "mem"), 0, 0, tiled=True)
            control = got.reshape(tiles, groups, own_levels, lat_rows, share, nlon)
            control = control.transpose(0, 4, 3, 1, 2, 5).reshape(
                tiles * share, lat_rows, levels, nlon
            )
        else:
            control = lax.all_to_all(control, "tile", split_axis=1, concat_axis=2, tiled=True)
            control = lax.all_to_all(control, "mem", split_axis=2, concat_axis=0, tiled=True)
            control = control.transpose(2, 1, 0, 3)
        return control

    local_cells = obs_cell[0]
    innov = innovations[0]
    weight = obs_weight[0]
    size = slots * lat_rows * shard_cols
    state_shape = (slots, own_levels, lat_rows, nlon)
    gathered = add_at_cells(local_cells, jnp.stack([weight * innov, weight], axis=1), size)
    gathered = gathered.reshape(slots, lat_rows, own_levels, nlon, 2).transpose(4, 0, 2, 1, 3)

    tables = jnp.zeros((lat_rows, nlon), jnp.float32)
    tables = tables.at[:, 0].set(row_start.astype(jnp.float32))
    tables = tables.at[:, 1].set(row_length.astype(jnp.float32))
    payload = jnp.concatenate(
        [gathered.reshape(2 * slots * own_levels, lat_rows, nlon), tables[None]], axis=0
    )
    payload = gather_rows_by_permutes(payload, 1)
    tables = payload[-1, :, :2].astype(jnp.int32)
    mask = row_mask(tables[:, 0], tables[:, 1], nlon)
    both = payload[:-1].reshape(2, slots, own_levels, tiles * lat_rows, nlon)
    first_grad, obs_diag = both[0], both[1]
    me = lax.axis_index("tile")

    residual = adjoint(first_grad, jnp.ones_like(first_grad))
    direction = residual
    control = jnp.zeros_like(residual)
    increment = jnp.zeros(state_shape, jnp.float32)
    norm_now = None
    for step in range(ITERS):
        state = forward(direction)
        image = direction + adjoint(obs_diag, state)
        if norm_now is None:
            sums = global_sum(jnp.stack([jnp.sum(residual * residual), jnp.sum(direction * image)]))
            norm_now, curvature = sums[0], sums[1]
        else:
            curvature = global_sum(jnp.sum(direction * image))
        alpha = norm_now / curvature
        control = control + alpha * direction
        own_state = lax.dynamic_slice_in_dim(state, me * lat_rows, lat_rows, axis=2)
        increment = increment + alpha * own_state
        if step + 1 < ITERS:
            residual = residual - alpha * image
            norm_next = global_sum(jnp.sum(residual * residual))
            direction = residual + norm_next / norm_now * direction
            norm_now = norm_next
    control = to_output(control)
    increment = increment.transpose(0, 2, 1, 3).reshape(slots, lat_rows, shard_cols)
    return (control, increment)


def solution(mesh):
    return jax.shard_map(
        body,
        mesh=mesh,
        in_specs=(
            P("mem", None, "tile", None, None),
            P("tile", "mem"),
            P("tile", "mem"),
            P("tile", "mem"),
            P("tile"),
            P("tile"),
            P(),
            P(),
        ),
        out_specs=(P("mem", "tile", None, None), P(None, "tile", "mem")),
        check_vma=False,
    )
```

```python
import jax
import jax.numpy as jnp
from jax import lax
from jax.experimental import pallas as pl
from jax.experimental.pallas import tpu as pltpu
from jax.sharding import PartitionSpec as P

ITERS = 2
STEPS = 8


def row_mask(starts, lengths, nlon):
    lon = lax.broadcasted_iota(jnp.int32, (starts.shape[0], nlon), 1)
    rel = (lon - starts[:, None]) % nlon
    return jnp.where(rel < lengths[:, None], 1.0, 0.0).astype(jnp.float32)[:, None, :]


def diffuse_step(field, mask, lat_rate, lon_rate):
    zero = jnp.zeros_like(field[:, :1])
    north = jnp.concatenate([field[:, 1:], zero], axis=1)
    south = jnp.concatenate([zero, field[:, :-1]], axis=1)
    east = jnp.roll(field, -1, axis=3)
    west = jnp.roll(field, 1, axis=3)
    lat_term = north + south - 2.0 * field
    lon_term = east + west - 2.0 * field
    return mask * (
        field + lat_rate[:, None, None, None] * lat_term + lon_rate[:, None, None, None] * lon_term
    )


def smooth_level(rates_ref, mask, now, level):
    rows, members, nlon = now.shape
    lat = rates_ref[0, level]
    lon = rates_ref[1, level]
    zero = jnp.zeros((1, members, nlon), jnp.float32)
    now = mask * now
    for inner in range(STEPS):
        north = jnp.concatenate([now[1:], zero], axis=0)
        south = jnp.concatenate([zero, now[:-1]], axis=0)
        east = pltpu.roll(now, nlon - 1, 2)
        west = pltpu.roll(now, 1, 2)
        lat_term = north + south - 2.0 * now
        lon_term = east + west - 2.0 * now
        now = mask * (now + lat * lat_term + lon * lon_term)
    return now


def adjoint_kernel(rates_ref, mask_ref, pert_ref, diag_ref, state_ref, out_ref):
    slots, levels = pert_ref.shape[:2]
    mask = mask_ref[...]
    for level in range(levels):
        field = None
        for slot in range(slots):
            grad = diag_ref[slot, level] * state_ref[slot, level]
            term = pert_ref[slot, level] * grad[:, None, :]
            field = term if field is None else field + term
        out_ref[level] = smooth_level(rates_ref, mask, field, level)


def forward_kernel(rates_ref, mask_ref, pert_ref, field_ref, out_ref):
    slots, levels = pert_ref.shape[:2]
    mask = mask_ref[...]
    for level in range(levels):
        smoothed = smooth_level(rates_ref, mask, field_ref[level], level)
        for slot in range(slots):
            out_ref[slot, level] = jnp.sum(pert_ref[slot, level] * smoothed, axis=1)


def local_call(kernel, out_shape, rates, *arrays):
    size = sum(a.size for a in arrays)
    return pl.pallas_call(
        kernel,
        out_shape=jax.ShapeDtypeStruct(out_shape, jnp.float32),
        in_specs=[pl.BlockSpec(memory_space=pltpu.SMEM)]
        + [pl.BlockSpec(memory_space=pltpu.VMEM)] * len(arrays),
        out_specs=pl.BlockSpec(memory_space=pltpu.VMEM),
        cost_estimate=pl.CostEstimate(
            flops=16 * STEPS * size, bytes_accessed=4 * size, transcendentals=0
        ),
    )(rates, *arrays)


def global_sum(value):
    axes = ("tile", "mem")
    count = lax.axis_size(axes)
    value = jnp.asarray(value, jnp.float32)
    spread = jnp.broadcast_to(value, (count,) + value.shape)
    return jnp.sum(lax.all_to_all(spread, axes, 0, 0, tiled=True), axis=0)


def add_at_cells(cells, values, size):
    lanes = 128
    count, kinds = values.shape
    high = lax.broadcasted_iota(jnp.int32, (count, size // lanes), 1) == (cells // lanes)[:, None]
    low = lax.broadcasted_iota(jnp.int32, (count, lanes), 1) == (cells % lanes)[:, None]
    spread = values[:, :, None] * low.astype(jnp.float32)[:, None, :]
    summed = jnp.dot(
        high.astype(jnp.float32).T,
        spread.reshape(count, kinds * lanes),
        precision=lax.Precision.HIGHEST,
        preferred_element_type=jnp.float32,
    )
    return summed.reshape(size // lanes, kinds, lanes).transpose(0, 2, 1).reshape(size, kinds)


def gather_rows(block, dim):
    count = lax.axis_size("tile")
    shape = block.shape
    copies = jnp.broadcast_to(
        jnp.expand_dims(block, dim), shape[:dim] + (count,) + shape[dim:]
    )
    joined = lax.all_to_all(copies, "tile", dim, dim, tiled=True)
    return joined.reshape(shape[:dim] + (count * shape[dim],) + shape[dim + 1 :])


def gather_rows_by_permutes(block, dim):
    count = lax.axis_size("tile")
    me = lax.axis_index("tile")
    pieces = [block] + [
        lax.ppermute(block, "tile", [(i, (i + k) % count) for i in range(count)])
        for k in range(1, count)
    ]
    by_offset = jnp.stack([pieces[(count - q) % count] for q in range(count)], axis=dim)
    ordered = jnp.roll(by_offset, me, axis=dim)
    shape = block.shape
    return ordered.reshape(shape[:dim] + (count * shape[dim],) + shape[dim + 1 :])


def reduce_rows_by_permutes(block, dim):
    count = lax.axis_size("tile")
    me = lax.axis_index("tile")
    share = block.shape[dim] // count
    total = lax.dynamic_slice_in_dim(block, me * share, share, axis=dim)
    for k in range(1, count):
        piece = lax.dynamic_slice_in_dim(block, ((me + k) % count) * share, share, axis=dim)
        total = total + lax.ppermute(piece, "tile", [(i, (i + k) % count) for i in range(count)])
    return total


def sum_over_tile_by_permutes(block):
    count = lax.axis_size("tile")
    total = block
    for k in range(1, count):
        total = total + lax.ppermute(block, "tile", [(i, (i + k) % count) for i in range(count)])
    return total


def reduce_rows(block, dim):
    count = lax.axis_size("tile")
    shape = block.shape
    parts = block.reshape(shape[:dim] + (count, shape[dim] // count) + shape[dim + 1 :])
    received = lax.all_to_all(parts, "tile", dim, dim, tiled=True)
    return jnp.sum(received, axis=dim)


def body(
    perturbations, innovations, obs_weight, obs_cell, row_start, row_length, lat_rate, lon_rate
):
    slots = perturbations.shape[1]
    lat_rows = perturbations.shape[2]
    levels = perturbations.shape[3]
    nlon = perturbations.shape[4]
    groups = lax.axis_size("mem")
    own_levels = levels // groups
    shard_cols = own_levels * nlon
    first = lax.axis_index("mem") * own_levels
    lat_own = lax.dynamic_slice_in_dim(lat_rate, first, own_levels)
    lon_own = lax.dynamic_slice_in_dim(lon_rate, first, own_levels)

    tiles = lax.axis_size("tile")
    local_members = perturbations.shape[0]
    share = local_members // tiles
    if share and local_members % tiles == 0:
        sent = perturbations.astype(jnp.float32).reshape(
            tiles, share, slots, lat_rows, groups, own_levels, nlon
        )
        sent = sent.transpose(0, 4, 2, 5, 3, 1, 6).reshape(
            tiles * groups, slots, own_levels, lat_rows, share, nlon
        )
        pert_levels = []
        for level in range(own_levels):
            got = lax.all_to_all(sent[:, :, level : level + 1], ("tile", "mem"), 0, 0, tiled=True)
            got = got.reshape(tiles, groups, slots, 1, lat_rows, share, nlon)
            pert_levels.append(
                got.transpose(2, 3, 0, 4, 1, 5, 6).reshape(
                    slots, 1, tiles * lat_rows, groups * share, nlon
                )
            )
        pert = jnp.concatenate(pert_levels, axis=1) if own_levels > 1 else pert_levels[0]
    else:
        pert = lax.all_to_all(
            perturbations.astype(jnp.float32).transpose(1, 3, 2, 0, 4),
            "mem",
            split_axis=1,
            concat_axis=3,
            tiled=True,
        )
        pert = lax.all_to_all(pert, "tile", split_axis=3, concat_axis=2, tiled=True)
        pert_levels = [pert[:, level : level + 1] for level in range(own_levels)]

    rates = jnp.stack([lat_own, lon_own])

    def forward(control, by_level=False):
        if by_level:
            parts = [
                local_call(
                    forward_kernel,
                    (slots, 1, control.shape[1], nlon),
                    rates[:, level : level + 1],
                    mask,
                    pert_levels[level],
                    control[level : level + 1],
                )
                for level in range(own_levels)
            ]
            partial = jnp.concatenate(parts, axis=1) if own_levels > 1 else parts[0]
        else:
            partial = local_call(
                forward_kernel,
                (slots, own_levels, control.shape[1], nlon),
                rates,
                mask,
                pert,
                control,
            )
        return sum_over_tile_by_permutes(partial)

    def adjoint(diag, state, by_level=False):
        if not by_level:
            return local_call(adjoint_kernel, pert.shape[1:], rates, mask, pert, diag, state)
        parts = [
            local_call(
                adjoint_kernel,
                (1,) + pert.shape[2:],
                rates[:, level : level + 1],
                mask,
                pert_levels[level],
                diag[:, level : level + 1],
                state[:, level : level + 1],
            )
            for level in range(own_levels)
        ]
        return jnp.concatenate(parts, axis=0) if own_levels > 1 else parts[0]

    def to_output(control):
        if share and local_members % tiles == 0:
            sent = control.reshape(own_levels, tiles, lat_rows, groups, share, nlon)
            sent = sent.transpose(1, 3, 0, 2, 4, 5).reshape(
                tiles * groups, own_levels, lat_rows, share, nlon
            )
            got = lax.all_to_all(sent, ("tile", "mem"), 0, 0, tiled=True)
            control = got.reshape(tiles, groups, own_levels, lat_rows, share, nlon)
            control = control.transpose(0, 4, 3, 1, 2, 5).reshape(
                tiles * share, lat_rows, levels, nlon
            )
        else:
            control = lax.all_to_all(control, "tile", split_axis=1, concat_axis=2, tiled=True)
            control = lax.all_to_all(control, "mem", split_axis=2, concat_axis=0, tiled=True)
            control = control.transpose(2, 1, 0, 3)
        return control

    local_cells = obs_cell[0]
    innov = innovations[0]
    weight = obs_weight[0]
    size = slots * lat_rows * shard_cols
    state_shape = (slots, own_levels, lat_rows, nlon)
    gathered = add_at_cells(local_cells, jnp.stack([weight * innov, weight], axis=1), size)
    gathered = gathered.reshape(slots, lat_rows, own_levels, nlon, 2).transpose(4, 0, 2, 1, 3)

    tables = jnp.zeros((lat_rows, nlon), jnp.float32)
    tables = tables.at[:, 0].set(row_start.astype(jnp.float32))
    tables = tables.at[:, 1].set(row_length.astype(jnp.float32))
    payload = jnp.concatenate(
        [gathered.reshape(2 * slots * own_levels, lat_rows, nlon), tables[None]], axis=0
    )
    payload = gather_rows_by_permutes(payload, 1)
    tables = payload[-1, :, :2].astype(jnp.int32)
    mask = row_mask(tables[:, 0], tables[:, 1], nlon)
    both = payload[:-1].reshape(2, slots, own_levels, tiles * lat_rows, nlon)
    first_grad, obs_diag = both[0], both[1]
    me = lax.axis_index("tile")

    residual = adjoint(first_grad, jnp.ones_like(first_grad), by_level=True)
    direction = residual
    control = jnp.zeros_like(residual)
    increment = jnp.zeros(state_shape, jnp.float32)
    norm_now = None
    for step in range(ITERS):
        state = forward(direction, by_level=step == 0)
        image = direction + adjoint(obs_diag, state)
        if norm_now is None:
            sums = global_sum(jnp.stack([jnp.sum(residual * residual), jnp.sum(direction * image)]))
            norm_now, curvature = sums[0], sums[1]
        else:
            curvature = global_sum(jnp.sum(direction * image))
        alpha = norm_now / curvature
        control = control + alpha * direction
        own_state = lax.dynamic_slice_in_dim(state, me * lat_rows, lat_rows, axis=2)
        increment = increment + alpha * own_state
        if step + 1 < ITERS:
            residual = residual - alpha * image
            norm_next = global_sum(jnp.sum(residual * residual))
            direction = residual + norm_next / norm_now * direction
            norm_now = norm_next
    control = to_output(control)
    increment = increment.transpose(0, 2, 1, 3).reshape(slots, lat_rows, shard_cols)
    return (control, increment)


def solution(mesh):
    return jax.shard_map(
        body,
        mesh=mesh,
        in_specs=(
            P("mem", None, "tile", None, None),
            P("tile", "mem"),
            P("tile", "mem"),
            P("tile", "mem"),
            P("tile"),
            P("tile"),
            P(),
            P(),
        ),
        out_specs=(P("mem", "tile", None, None), P(None, "tile", "mem")),
        check_vma=False,
    )
```

```python
import jax
import jax.numpy as jnp
from jax import lax
from jax.experimental import pallas as pl
from jax.experimental.pallas import tpu as pltpu
from jax.sharding import PartitionSpec as P

ITERS = 2
STEPS = 8


def row_mask(starts, lengths, nlon):
    lon = lax.broadcasted_iota(jnp.int32, (starts.shape[0], nlon), 1)
    rel = (lon - starts[:, None]) % nlon
    return jnp.where(rel < lengths[:, None], 1.0, 0.0).astype(jnp.float32)[:, None, :]


def diffuse_step(field, mask, lat_rate, lon_rate):
    zero = jnp.zeros_like(field[:, :1])
    north = jnp.concatenate([field[:, 1:], zero], axis=1)
    south = jnp.concatenate([zero, field[:, :-1]], axis=1)
    east = jnp.roll(field, -1, axis=3)
    west = jnp.roll(field, 1, axis=3)
    lat_term = north + south - 2.0 * field
    lon_term = east + west - 2.0 * field
    return mask * (
        field + lat_rate[:, None, None, None] * lat_term + lon_rate[:, None, None, None] * lon_term
    )


def smooth_level(rates_ref, mask, now, level):
    rows, members, nlon = now.shape
    lat = rates_ref[0, level]
    lon = rates_ref[1, level]
    zero = jnp.zeros((1, members, nlon), jnp.float32)
    now = mask * now
    for inner in range(STEPS):
        north = jnp.concatenate([now[1:], zero], axis=0)
        south = jnp.concatenate([zero, now[:-1]], axis=0)
        east = pltpu.roll(now, nlon - 1, 2)
        west = pltpu.roll(now, 1, 2)
        lat_term = north + south - 2.0 * now
        lon_term = east + west - 2.0 * now
        now = mask * (now + lat * lat_term + lon * lon_term)
    return now


def adjoint_kernel(rates_ref, mask_ref, pert_ref, diag_ref, *refs):
    pieces, out_ref = refs[:-1], refs[-1]
    slots, levels = pert_ref.shape[:2]
    mask = mask_ref[...]
    for level in range(levels):
        field = None
        for slot in range(slots):
            state = pieces[0][slot, level]
            for piece in pieces[1:]:
                state = state + piece[slot, level]
            grad = diag_ref[slot, level] * state
            term = pert_ref[slot, level] * grad[:, None, :]
            field = term if field is None else field + term
        out_ref[level] = smooth_level(rates_ref, mask, field, level)


def forward_kernel(rates_ref, mask_ref, pert_ref, field_ref, out_ref):
    slots, levels = pert_ref.shape[:2]
    mask = mask_ref[...]
    for level in range(levels):
        smoothed = smooth_level(rates_ref, mask, field_ref[level], level)
        for slot in range(slots):
            out_ref[slot, level] = jnp.sum(pert_ref[slot, level] * smoothed, axis=1)


def local_call(kernel, out_shape, rates, *arrays):
    size = sum(a.size for a in arrays)
    return pl.pallas_call(
        kernel,
        out_shape=jax.ShapeDtypeStruct(out_shape, jnp.float32),
        in_specs=[pl.BlockSpec(memory_space=pltpu.SMEM)]
        + [pl.BlockSpec(memory_space=pltpu.VMEM)] * len(arrays),
        out_specs=pl.BlockSpec(memory_space=pltpu.VMEM),
        cost_estimate=pl.CostEstimate(
            flops=16 * STEPS * size, bytes_accessed=4 * size, transcendentals=0
        ),
    )(rates, *arrays)


def global_sum(value):
    axes = ("tile", "mem")
    count = lax.axis_size(axes)
    value = jnp.asarray(value, jnp.float32)
    spread = jnp.broadcast_to(value, (count,) + value.shape)
    return jnp.sum(lax.all_to_all(spread, axes, 0, 0, tiled=True), axis=0)


def add_at_cells(cells, values, size):
    lanes = 128
    count, kinds = values.shape
    high = lax.broadcasted_iota(jnp.int32, (count, size // lanes), 1) == (cells // lanes)[:, None]
    low = lax.broadcasted_iota(jnp.int32, (count, lanes), 1) == (cells % lanes)[:, None]
    spread = values[:, :, None] * low.astype(jnp.float32)[:, None, :]
    summed = jnp.dot(
        high.astype(jnp.float32).T,
        spread.reshape(count, kinds * lanes),
        precision=lax.Precision.HIGHEST,
        preferred_element_type=jnp.float32,
    )
    return summed.reshape(size // lanes, kinds, lanes).transpose(0, 2, 1).reshape(size, kinds)


def gather_rows(block, dim):
    count = lax.axis_size("tile")
    shape = block.shape
    copies = jnp.broadcast_to(
        jnp.expand_dims(block, dim), shape[:dim] + (count,) + shape[dim:]
    )
    joined = lax.all_to_all(copies, "tile", dim, dim, tiled=True)
    return joined.reshape(shape[:dim] + (count * shape[dim],) + shape[dim + 1 :])


def gather_rows_by_permutes(block, dim):
    count = lax.axis_size("tile")
    me = lax.axis_index("tile")
    pieces = [block] + [
        lax.ppermute(block, "tile", [(i, (i + k) % count) for i in range(count)])
        for k in range(1, count)
    ]
    by_offset = jnp.stack([pieces[(count - q) % count] for q in range(count)], axis=dim)
    ordered = jnp.roll(by_offset, me, axis=dim)
    shape = block.shape
    return ordered.reshape(shape[:dim] + (count * shape[dim],) + shape[dim + 1 :])


def reduce_rows_by_permutes(block, dim):
    count = lax.axis_size("tile")
    me = lax.axis_index("tile")
    share = block.shape[dim] // count
    total = lax.dynamic_slice_in_dim(block, me * share, share, axis=dim)
    for k in range(1, count):
        piece = lax.dynamic_slice_in_dim(block, ((me + k) % count) * share, share, axis=dim)
        total = total + lax.ppermute(piece, "tile", [(i, (i + k) % count) for i in range(count)])
    return total


def pieces_over_tile(block):
    count = lax.axis_size("tile")
    return [block] + [
        lax.ppermute(block, "tile", [(i, (i + k) % count) for i in range(count)])
        for k in range(1, count)
    ]


def reduce_rows(block, dim):
    count = lax.axis_size("tile")
    shape = block.shape
    parts = block.reshape(shape[:dim] + (count, shape[dim] // count) + shape[dim + 1 :])
    received = lax.all_to_all(parts, "tile", dim, dim, tiled=True)
    return jnp.sum(received, axis=dim)


def body(
    perturbations, innovations, obs_weight, obs_cell, row_start, row_length, lat_rate, lon_rate
):
    slots = perturbations.shape[1]
    lat_rows = perturbations.shape[2]
    levels = perturbations.shape[3]
    nlon = perturbations.shape[4]
    groups = lax.axis_size("mem")
    own_levels = levels // groups
    shard_cols = own_levels * nlon
    first = lax.axis_index("mem") * own_levels
    lat_own = lax.dynamic_slice_in_dim(lat_rate, first, own_levels)
    lon_own = lax.dynamic_slice_in_dim(lon_rate, first, own_levels)

    tiles = lax.axis_size("tile")
    local_members = perturbations.shape[0]
    share = local_members // tiles
    if share and local_members % tiles == 0:
        sent = perturbations.astype(jnp.float32).reshape(
            tiles, share, slots, lat_rows, groups, own_levels, nlon
        )
        sent = sent.transpose(0, 4, 2, 5, 3, 1, 6).reshape(
            tiles * groups, slots, own_levels, lat_rows, share, nlon
        )
        got = lax.all_to_all(sent, ("tile", "mem"), 0, 0, tiled=True)
        pert = got.reshape(tiles, groups, slots, own_levels, lat_rows, share, nlon)
        pert = pert.transpose(2, 3, 0, 4, 1, 5, 6).reshape(
            slots, own_levels, tiles * lat_rows, groups * share, nlon
        )
    else:
        pert = lax.all_to_all(
            perturbations.astype(jnp.float32).transpose(1, 3, 2, 0, 4),
            "mem",
            split_axis=1,
            concat_axis=3,
            tiled=True,
        )
        pert = lax.all_to_all(pert, "tile", split_axis=3, concat_axis=2, tiled=True)

    rates = jnp.stack([lat_own, lon_own])

    def forward(control):
        partial = local_call(
            forward_kernel,
            (slots, own_levels, control.shape[1], nlon),
            rates,
            mask,
            pert,
            control,
        )
        return pieces_over_tile(partial)

    def adjoint(diag, pieces):
        return local_call(adjoint_kernel, pert.shape[1:], rates, mask, pert, diag, *pieces)

    def to_output(control):
        if share and local_members % tiles == 0:
            sent = control.reshape(own_levels, tiles, lat_rows, groups, share, nlon)
            sent = sent.transpose(1, 3, 0, 2, 4, 5).reshape(
                tiles * groups, own_levels, lat_rows, share, nlon
            )
            got = lax.all_to_all(sent, ("tile", "mem"), 0, 0, tiled=True)
            control = got.reshape(tiles, groups, own_levels, lat_rows, share, nlon)
            control = control.transpose(0, 4, 3, 1, 2, 5).reshape(
                tiles * share, lat_rows, levels, nlon
            )
        else:
            control = lax.all_to_all(control, "tile", split_axis=1, concat_axis=2, tiled=True)
            control = lax.all_to_all(control, "mem", split_axis=2, concat_axis=0, tiled=True)
            control = control.transpose(2, 1, 0, 3)
        return control

    local_cells = obs_cell[0]
    innov = innovations[0]
    weight = obs_weight[0]
    size = slots * lat_rows * shard_cols
    state_shape = (slots, own_levels, lat_rows, nlon)
    gathered = add_at_cells(local_cells, jnp.stack([weight * innov, weight], axis=1), size)
    gathered = gathered.reshape(slots, lat_rows, own_levels, nlon, 2).transpose(4, 0, 2, 1, 3)

    tables = jnp.zeros((lat_rows, nlon), jnp.float32)
    tables = tables.at[:, 0].set(row_start.astype(jnp.float32))
    tables = tables.at[:, 1].set(row_length.astype(jnp.float32))
    payload = jnp.concatenate(
        [gathered.reshape(2 * slots * own_levels, lat_rows, nlon), tables[None]], axis=0
    )
    payload = gather_rows_by_permutes(payload, 1)
    tables = payload[-1, :, :2].astype(jnp.int32)
    mask = row_mask(tables[:, 0], tables[:, 1], nlon)
    both = payload[:-1].reshape(2, slots, own_levels, tiles * lat_rows, nlon)
    first_grad, obs_diag = both[0], both[1]
    me = lax.axis_index("tile")

    residual = adjoint(first_grad, [jnp.ones_like(first_grad)])
    direction = residual
    control = jnp.zeros_like(residual)
    increment = jnp.zeros(state_shape, jnp.float32)
    norm_now = None
    for step in range(ITERS):
        state = forward(direction)
        image = direction + adjoint(obs_diag, state)
        if norm_now is None:
            sums = global_sum(jnp.stack([jnp.sum(residual * residual), jnp.sum(direction * image)]))
            norm_now, curvature = sums[0], sums[1]
        else:
            curvature = global_sum(jnp.sum(direction * image))
        alpha = norm_now / curvature
        control = control + alpha * direction
        own_state = None
        for piece in state:
            own = lax.dynamic_slice_in_dim(piece, me * lat_rows, lat_rows, axis=2)
            own_state = own if own_state is None else own_state + own
        increment = increment + alpha * own_state
        if step + 1 < ITERS:
            residual = residual - alpha * image
            norm_next = global_sum(jnp.sum(residual * residual))
            direction = residual + norm_next / norm_now * direction
            norm_now = norm_next
    control = to_output(control)
    increment = increment.transpose(0, 2, 1, 3).reshape(slots, lat_rows, shard_cols)
    return (control, increment)


def solution(mesh):
    return jax.shard_map(
        body,
        mesh=mesh,
        in_specs=(
            P("mem", None, "tile", None, None),
            P("tile", "mem"),
            P("tile", "mem"),
            P("tile", "mem"),
            P("tile"),
            P("tile"),
            P(),
            P(),
        ),
        out_specs=(P("mem", "tile", None, None), P(None, "tile", "mem")),
        check_vma=False,
    )
```

```python
import jax
import jax.numpy as jnp
from jax import lax
from jax.experimental import pallas as pl
from jax.experimental.pallas import tpu as pltpu
from jax.sharding import PartitionSpec as P

ITERS = 2
STEPS = 8


def row_mask(starts, lengths, nlon):
    lon = lax.broadcasted_iota(jnp.int32, (starts.shape[0], nlon), 1)
    rel = (lon - starts[:, None]) % nlon
    return jnp.where(rel < lengths[:, None], 1.0, 0.0).astype(jnp.float32)[:, None, :]


def diffuse_step(field, mask, lat_rate, lon_rate):
    zero = jnp.zeros_like(field[:, :1])
    north = jnp.concatenate([field[:, 1:], zero], axis=1)
    south = jnp.concatenate([zero, field[:, :-1]], axis=1)
    east = jnp.roll(field, -1, axis=3)
    west = jnp.roll(field, 1, axis=3)
    lat_term = north + south - 2.0 * field
    lon_term = east + west - 2.0 * field
    return mask * (
        field + lat_rate[:, None, None, None] * lat_term + lon_rate[:, None, None, None] * lon_term
    )


def smooth_level(rates_ref, mask, now, level):
    rows, members, nlon = now.shape
    lat = rates_ref[0, level]
    lon = rates_ref[1, level]
    zero = jnp.zeros((1, members, nlon), jnp.float32)
    now = mask * now
    for inner in range(STEPS):
        north = jnp.concatenate([now[1:], zero], axis=0)
        south = jnp.concatenate([zero, now[:-1]], axis=0)
        east = pltpu.roll(now, nlon - 1, 2)
        west = pltpu.roll(now, 1, 2)
        lat_term = north + south - 2.0 * now
        lon_term = east + west - 2.0 * now
        now = mask * (now + lat * lat_term + lon * lon_term)
    return now


def adjoint_kernel(rates_ref, mask_ref, pert_ref, diag_ref, state_ref, out_ref):
    slots, levels = pert_ref.shape[:2]
    mask = mask_ref[...]
    for level in range(levels):
        field = None
        for slot in range(slots):
            grad = diag_ref[slot, level] * state_ref[slot, level]
            term = pert_ref[slot, level] * grad[:, None, :]
            field = term if field is None else field + term
        out_ref[level] = smooth_level(rates_ref, mask, field, level)


def forward_kernel(rates_ref, mask_ref, pert_ref, field_ref, out_ref):
    slots, levels = pert_ref.shape[:2]
    mask = mask_ref[...]
    for level in range(levels):
        smoothed = smooth_level(rates_ref, mask, field_ref[level], level)
        for slot in range(slots):
            out_ref[slot, level] = jnp.sum(pert_ref[slot, level] * smoothed, axis=1)


def local_call(kernel, out_shape, rates, *arrays):
    size = sum(a.size for a in arrays)
    return pl.pallas_call(
        kernel,
        out_shape=jax.ShapeDtypeStruct(out_shape, jnp.float32),
        in_specs=[pl.BlockSpec(memory_space=pltpu.SMEM)]
        + [pl.BlockSpec(memory_space=pltpu.VMEM)] * len(arrays),
        out_specs=pl.BlockSpec(memory_space=pltpu.VMEM),
        cost_estimate=pl.CostEstimate(
            flops=16 * STEPS * size, bytes_accessed=4 * size, transcendentals=0
        ),
    )(rates, *arrays)


def global_sum(value):
    axes = ("tile", "mem")
    count = lax.axis_size(axes)
    value = jnp.asarray(value, jnp.float32)
    spread = jnp.broadcast_to(value, (count,) + value.shape)
    return jnp.sum(lax.all_to_all(spread, axes, 0, 0, tiled=True), axis=0)


def add_at_cells(cells, values, size):
    lanes = 128
    count, kinds = values.shape
    high = lax.broadcasted_iota(jnp.int32, (count, size // lanes), 1) == (cells // lanes)[:, None]
    low = lax.broadcasted_iota(jnp.int32, (count, lanes), 1) == (cells % lanes)[:, None]
    spread = values[:, :, None] * low.astype(jnp.float32)[:, None, :]
    summed = jnp.dot(
        high.astype(jnp.float32).T,
        spread.reshape(count, kinds * lanes),
        precision=lax.Precision.HIGHEST,
        preferred_element_type=jnp.float32,
    )
    return summed.reshape(size // lanes, kinds, lanes).transpose(0, 2, 1).reshape(size, kinds)


def gather_rows(block, dim):
    count = lax.axis_size("tile")
    shape = block.shape
    copies = jnp.broadcast_to(
        jnp.expand_dims(block, dim), shape[:dim] + (count,) + shape[dim:]
    )
    joined = lax.all_to_all(copies, "tile", dim, dim, tiled=True)
    return joined.reshape(shape[:dim] + (count * shape[dim],) + shape[dim + 1 :])


def gather_rows_by_permutes(block, dim):
    count = lax.axis_size("tile")
    me = lax.axis_index("tile")
    pieces = [block] + [
        lax.ppermute(block, "tile", [(i, (i + k) % count) for i in range(count)])
        for k in range(1, count)
    ]
    by_offset = jnp.stack([pieces[(count - q) % count] for q in range(count)], axis=dim)
    ordered = jnp.roll(by_offset, me, axis=dim)
    shape = block.shape
    return ordered.reshape(shape[:dim] + (count * shape[dim],) + shape[dim + 1 :])


def reduce_rows_by_permutes(block, dim):
    count = lax.axis_size("tile")
    me = lax.axis_index("tile")
    share = block.shape[dim] // count
    total = lax.dynamic_slice_in_dim(block, me * share, share, axis=dim)
    for k in range(1, count):
        piece = lax.dynamic_slice_in_dim(block, ((me + k) % count) * share, share, axis=dim)
        total = total + lax.ppermute(piece, "tile", [(i, (i + k) % count) for i in range(count)])
    return total


def sum_over_tile_by_permutes(block):
    count = lax.axis_size("tile")
    total = block
    for k in range(1, count):
        total = total + lax.ppermute(block, "tile", [(i, (i + k) % count) for i in range(count)])
    return total


def reduce_rows(block, dim):
    count = lax.axis_size("tile")
    shape = block.shape
    parts = block.reshape(shape[:dim] + (count, shape[dim] // count) + shape[dim + 1 :])
    received = lax.all_to_all(parts, "tile", dim, dim, tiled=True)
    return jnp.sum(received, axis=dim)


def body(
    perturbations, innovations, obs_weight, obs_cell, row_start, row_length, lat_rate, lon_rate
):
    slots = perturbations.shape[1]
    lat_rows = perturbations.shape[2]
    levels = perturbations.shape[3]
    nlon = perturbations.shape[4]
    groups = lax.axis_size("mem")
    own_levels = levels // groups
    shard_cols = own_levels * nlon
    first = lax.axis_index("mem") * own_levels
    lat_own = lax.dynamic_slice_in_dim(lat_rate, first, own_levels)
    lon_own = lax.dynamic_slice_in_dim(lon_rate, first, own_levels)

    tiles = lax.axis_size("tile")
    local_members = perturbations.shape[0]
    share = local_members // tiles
    if share and local_members % tiles == 0:
        sent = perturbations.astype(jnp.float32).reshape(
            tiles, share, slots, lat_rows, groups, own_levels, nlon
        )
        sent = sent.transpose(0, 4, 2, 5, 3, 1, 6).reshape(
            tiles * groups, slots, own_levels, lat_rows, share, nlon
        )
        got = lax.all_to_all(sent, ("tile", "mem"), 0, 0, tiled=True)
        pert = got.reshape(tiles, groups, slots, own_levels, lat_rows, share, nlon)
        pert = pert.transpose(2, 3, 0, 4, 1, 5, 6).reshape(
            slots, own_levels, tiles * lat_rows, groups * share, nlon
        )
    else:
        pert = lax.all_to_all(
            perturbations.astype(jnp.float32).transpose(1, 3, 2, 0, 4),
            "mem",
            split_axis=1,
            concat_axis=3,
            tiled=True,
        )
        pert = lax.all_to_all(pert, "tile", split_axis=3, concat_axis=2, tiled=True)

    rates = jnp.stack([lat_own, lon_own])

    def forward(control):
        partial = local_call(
            forward_kernel,
            (slots, own_levels, control.shape[1], nlon),
            rates,
            mask,
            pert,
            control,
        )
        return sum_over_tile_by_permutes(partial)

    def adjoint(diag, state):
        return local_call(
            adjoint_kernel, pert.shape[1:], rates, mask, pert, diag, state
        )

    def to_output(control):
        if share and local_members % tiles == 0:
            sent = control.reshape(own_levels, tiles, lat_rows, groups, share, nlon)
            sent = sent.transpose(1, 3, 0, 2, 4, 5).reshape(
                tiles * groups, own_levels, lat_rows, share, nlon
            )
            got = lax.all_to_all(sent, ("tile", "mem"), 0, 0, tiled=True)
            control = got.reshape(tiles, groups, own_levels, lat_rows, share, nlon)
            control = control.transpose(0, 4, 3, 1, 2, 5).reshape(
                tiles * share, lat_rows, levels, nlon
            )
        else:
            control = lax.all_to_all(control, "tile", split_axis=1, concat_axis=2, tiled=True)
            control = lax.all_to_all(control, "mem", split_axis=2, concat_axis=0, tiled=True)
            control = control.transpose(2, 1, 0, 3)
        return control

    local_cells = obs_cell[0]
    innov = innovations[0]
    weight = obs_weight[0]
    size = slots * lat_rows * shard_cols
    state_shape = (slots, own_levels, lat_rows, nlon)
    gathered = add_at_cells(local_cells, jnp.stack([weight * innov, weight], axis=1), size)
    gathered = gathered.reshape(slots, lat_rows, own_levels, nlon, 2).transpose(4, 0, 2, 1, 3)

    tables = jnp.zeros((lat_rows, nlon), jnp.float32)
    tables = tables.at[:, 0].set(row_start.astype(jnp.float32))
    tables = tables.at[:, 1].set(row_length.astype(jnp.float32))
    payload = jnp.concatenate(
        [gathered.reshape(2 * slots * own_levels, lat_rows, nlon), tables[None]], axis=0
    )
    payload = gather_rows_by_permutes(payload, 1)
    tables = payload[-1, :, :2].astype(jnp.int32)
    mask = row_mask(tables[:, 0], tables[:, 1], nlon)
    both = payload[:-1].reshape(2, slots, own_levels, tiles * lat_rows, nlon)
    first_grad, obs_diag = both[0], both[1]
    me = lax.axis_index("tile")

    residual = adjoint(first_grad, jnp.ones_like(first_grad))
    direction = residual
    control = jnp.zeros_like(residual)
    increment = jnp.zeros(state_shape, jnp.float32)
    norm_now = None
    for step in range(ITERS):
        state = forward(direction)
        own_state = lax.dynamic_slice_in_dim(state, me * lat_rows, lat_rows, axis=2)
        if step + 1 < ITERS:
            image = direction + adjoint(obs_diag, state)
            dot = jnp.sum(direction * image)
        else:
            own_diag = lax.dynamic_slice_in_dim(obs_diag, me * lat_rows, lat_rows, axis=2)
            dot = jnp.sum(direction * direction) + jnp.sum(own_diag * own_state * own_state)
        if norm_now is None:
            sums = global_sum(jnp.stack([jnp.sum(residual * residual), dot]))
            norm_now, curvature = sums[0], sums[1]
        else:
            curvature = global_sum(dot)
        alpha = norm_now / curvature
        control = control + alpha * direction
        increment = increment + alpha * own_state
        if step + 1 < ITERS:
            residual = residual - alpha * image
            norm_next = global_sum(jnp.sum(residual * residual))
            direction = residual + norm_next / norm_now * direction
            norm_now = norm_next
    control = to_output(control)
    increment = increment.transpose(0, 2, 1, 3).reshape(slots, lat_rows, shard_cols)
    return (control, increment)


def solution(mesh):
    return jax.shard_map(
        body,
        mesh=mesh,
        in_specs=(
            P("mem", None, "tile", None, None),
            P("tile", "mem"),
            P("tile", "mem"),
            P("tile", "mem"),
            P("tile"),
            P("tile"),
            P(),
            P(),
        ),
        out_specs=(P("mem", "tile", None, None), P(None, "tile", "mem")),
        check_vma=False,
    )
```

```python
import jax
import jax.numpy as jnp
from jax import lax
from jax.experimental import pallas as pl
from jax.experimental.pallas import tpu as pltpu
from jax.sharding import PartitionSpec as P

ITERS = 2
STEPS = 8


def row_mask(starts, lengths, nlon):
    lon = lax.broadcasted_iota(jnp.int32, (starts.shape[0], nlon), 1)
    rel = (lon - starts[:, None]) % nlon
    return jnp.where(rel < lengths[:, None], 1.0, 0.0).astype(jnp.float32)[:, None, :]


def diffuse_step(field, mask, lat_rate, lon_rate):
    zero = jnp.zeros_like(field[:, :1])
    north = jnp.concatenate([field[:, 1:], zero], axis=1)
    south = jnp.concatenate([zero, field[:, :-1]], axis=1)
    east = jnp.roll(field, -1, axis=3)
    west = jnp.roll(field, 1, axis=3)
    lat_term = north + south - 2.0 * field
    lon_term = east + west - 2.0 * field
    return mask * (
        field + lat_rate[:, None, None, None] * lat_term + lon_rate[:, None, None, None] * lon_term
    )


def smooth_level(rates_ref, mask, now, level):
    rows, members, nlon = now.shape
    lat = rates_ref[0, level]
    lon = rates_ref[1, level]
    zero = jnp.zeros((1, members, nlon), jnp.float32)
    now = mask * now
    for inner in range(STEPS):
        north = jnp.concatenate([now[1:], zero], axis=0)
        south = jnp.concatenate([zero, now[:-1]], axis=0)
        east = pltpu.roll(now, nlon - 1, 2)
        west = pltpu.roll(now, 1, 2)
        lat_term = north + south - 2.0 * now
        lon_term = east + west - 2.0 * now
        now = mask * (now + lat * lat_term + lon * lon_term)
    return now


def adjoint_kernel(rates_ref, mask_ref, pert_ref, diag_ref, state_ref, out_ref):
    slots, levels = pert_ref.shape[:2]
    mask = mask_ref[...]
    for level in range(levels):
        field = None
        for slot in range(slots):
            grad = diag_ref[slot, level] * state_ref[slot, level]
            term = pert_ref[slot, level] * grad[:, None, :]
            field = term if field is None else field + term
        out_ref[level] = smooth_level(rates_ref, mask, field, level)


def forward_kernel(rates_ref, mask_ref, pert_ref, field_ref, out_ref):
    slots, levels = pert_ref.shape[:2]
    mask = mask_ref[...]
    for level in range(levels):
        smoothed = smooth_level(rates_ref, mask, field_ref[level], level)
        for slot in range(slots):
            out_ref[slot, level] = jnp.sum(pert_ref[slot, level] * smoothed, axis=1)


def local_call(kernel, out_shape, rates, *arrays):
    size = sum(a.size for a in arrays)
    return pl.pallas_call(
        kernel,
        out_shape=jax.ShapeDtypeStruct(out_shape, jnp.float32),
        in_specs=[pl.BlockSpec(memory_space=pltpu.SMEM)]
        + [pl.BlockSpec(memory_space=pltpu.VMEM)] * len(arrays),
        out_specs=pl.BlockSpec(memory_space=pltpu.VMEM),
        cost_estimate=pl.CostEstimate(
            flops=16 * STEPS * size, bytes_accessed=4 * size, transcendentals=0
        ),
    )(rates, *arrays)


def global_sum(value):
    axes = ("tile", "mem")
    count = lax.axis_size(axes)
    value = jnp.asarray(value, jnp.float32)
    spread = jnp.broadcast_to(value, (count,) + value.shape)
    return jnp.sum(lax.all_to_all(spread, axes, 0, 0, tiled=True), axis=0)


def add_at_cells(cells, values, size):
    lanes = 128
    count, kinds = values.shape
    high = lax.broadcasted_iota(jnp.int32, (count, size // lanes), 1) == (cells // lanes)[:, None]
    low = lax.broadcasted_iota(jnp.int32, (count, lanes), 1) == (cells % lanes)[:, None]
    spread = values[:, :, None] * low.astype(jnp.float32)[:, None, :]
    summed = jnp.dot(
        high.astype(jnp.float32).T,
        spread.reshape(count, kinds * lanes),
        precision=lax.Precision.HIGHEST,
        preferred_element_type=jnp.float32,
    )
    return summed.reshape(size // lanes, kinds, lanes).transpose(0, 2, 1).reshape(size, kinds)


def gather_rows(block, dim):
    count = lax.axis_size("tile")
    shape = block.shape
    copies = jnp.broadcast_to(
        jnp.expand_dims(block, dim), shape[:dim] + (count,) + shape[dim:]
    )
    joined = lax.all_to_all(copies, "tile", dim, dim, tiled=True)
    return joined.reshape(shape[:dim] + (count * shape[dim],) + shape[dim + 1 :])


def gather_rows_by_permutes(block, dim):
    count = lax.axis_size("tile")
    me = lax.axis_index("tile")
    pieces = [block] + [
        lax.ppermute(block, "tile", [(i, (i + k) % count) for i in range(count)])
        for k in range(1, count)
    ]
    by_offset = jnp.stack([pieces[(count - q) % count] for q in range(count)], axis=dim)
    ordered = jnp.roll(by_offset, me, axis=dim)
    shape = block.shape
    return ordered.reshape(shape[:dim] + (count * shape[dim],) + shape[dim + 1 :])


def reduce_rows_by_permutes(block, dim):
    count = lax.axis_size("tile")
    me = lax.axis_index("tile")
    share = block.shape[dim] // count
    total = lax.dynamic_slice_in_dim(block, me * share, share, axis=dim)
    for k in range(1, count):
        piece = lax.dynamic_slice_in_dim(block, ((me + k) % count) * share, share, axis=dim)
        total = total + lax.ppermute(piece, "tile", [(i, (i + k) % count) for i in range(count)])
    return total


def sum_over_tile_by_permutes(block):
    count = lax.axis_size("tile")
    total = block
    for k in range(1, count):
        total = total + lax.ppermute(block, "tile", [(i, (i + k) % count) for i in range(count)])
    return total


def reduce_rows(block, dim):
    count = lax.axis_size("tile")
    shape = block.shape
    parts = block.reshape(shape[:dim] + (count, shape[dim] // count) + shape[dim + 1 :])
    received = lax.all_to_all(parts, "tile", dim, dim, tiled=True)
    return jnp.sum(received, axis=dim)


def body(
    perturbations, innovations, obs_weight, obs_cell, row_start, row_length, lat_rate, lon_rate
):
    slots = perturbations.shape[1]
    lat_rows = perturbations.shape[2]
    levels = perturbations.shape[3]
    nlon = perturbations.shape[4]
    groups = lax.axis_size("mem")
    own_levels = levels // groups
    shard_cols = own_levels * nlon
    first = lax.axis_index("mem") * own_levels
    lat_own = lax.dynamic_slice_in_dim(lat_rate, first, own_levels)
    lon_own = lax.dynamic_slice_in_dim(lon_rate, first, own_levels)

    tiles = lax.axis_size("tile")
    local_members = perturbations.shape[0]
    share = local_members // tiles
    if share and local_members % tiles == 0:
        sent = perturbations.astype(jnp.float32).reshape(
            tiles, share, slots, lat_rows, groups, own_levels, nlon
        )
        sent = sent.transpose(0, 4, 2, 5, 3, 1, 6).reshape(
            tiles * groups, slots, own_levels, lat_rows, share, nlon
        )
        got = lax.all_to_all(sent, ("tile", "mem"), 0, 0, tiled=True)
        pert = got.reshape(tiles, groups, slots, own_levels, lat_rows, share, nlon)
        pert = pert.transpose(2, 3, 0, 4, 1, 5, 6).reshape(
            slots, own_levels, tiles * lat_rows, groups * share, nlon
        )
    else:
        pert = lax.all_to_all(
            perturbations.astype(jnp.float32).transpose(1, 3, 2, 0, 4),
            "mem",
            split_axis=1,
            concat_axis=3,
            tiled=True,
        )
        pert = lax.all_to_all(pert, "tile", split_axis=3, concat_axis=2, tiled=True)

    rates = jnp.stack([lat_own, lon_own])

    def forward(control):
        partial = local_call(
            forward_kernel,
            (slots, own_levels, control.shape[1], nlon),
            rates,
            mask,
            pert,
            control,
        )
        return sum_over_tile_by_permutes(partial)

    def adjoint(diag, state):
        return local_call(
            adjoint_kernel, pert.shape[1:], rates, mask, pert, diag, state
        )

    def to_output(control):
        if share and local_members % tiles == 0:
            sent = control.reshape(own_levels, tiles, lat_rows, groups, share, nlon)
            sent = sent.transpose(1, 3, 0, 2, 4, 5).reshape(
                tiles * groups, own_levels, lat_rows, share, nlon
            )
            got = lax.all_to_all(sent, ("tile", "mem"), 0, 0, tiled=True)
            control = got.reshape(tiles, groups, own_levels, lat_rows, share, nlon)
            control = control.transpose(0, 4, 3, 1, 2, 5).reshape(
                tiles * share, lat_rows, levels, nlon
            )
        else:
            control = lax.all_to_all(control, "tile", split_axis=1, concat_axis=2, tiled=True)
            control = lax.all_to_all(control, "mem", split_axis=2, concat_axis=0, tiled=True)
            control = control.transpose(2, 1, 0, 3)
        return control

    local_cells = obs_cell[0]
    innov = innovations[0]
    weight = obs_weight[0]
    size = slots * lat_rows * shard_cols
    state_shape = (slots, own_levels, lat_rows, nlon)
    gathered = add_at_cells(local_cells, jnp.stack([weight * innov, weight], axis=1), size)
    gathered = gathered.reshape(slots, lat_rows, own_levels, nlon, 2).transpose(4, 0, 2, 1, 3)

    tables = jnp.zeros((lat_rows, nlon), jnp.float32)
    tables = tables.at[:, 0].set(row_start.astype(jnp.float32))
    tables = tables.at[:, 1].set(row_length.astype(jnp.float32))
    payload = jnp.concatenate(
        [gathered.reshape(2 * slots * own_levels, lat_rows, nlon), tables[None]], axis=0
    )
    payload = gather_rows_by_permutes(payload, 1)
    tables = payload[-1, :, :2].astype(jnp.int32)
    mask = row_mask(tables[:, 0], tables[:, 1], nlon)
    both = payload[:-1].reshape(2, slots, own_levels, tiles * lat_rows, nlon)
    first_grad, obs_diag = both[0], both[1]
    me = lax.axis_index("tile")

    residual = adjoint(first_grad, jnp.ones_like(first_grad))
    direction = residual
    control = jnp.zeros_like(residual)
    increment = jnp.zeros(state_shape, jnp.float32)
    norm_now = None
    ahead = None
    for step in range(ITERS):
        if ahead is None:
            state = forward(direction)
        else:
            state = ahead[0] + ahead[1] * ahead[2]
        own_state = lax.dynamic_slice_in_dim(state, me * lat_rows, lat_rows, axis=2)
        if step + 1 < ITERS:
            image = direction + adjoint(obs_diag, state)
            dot = jnp.sum(direction * image)
        else:
            own_diag = lax.dynamic_slice_in_dim(obs_diag, me * lat_rows, lat_rows, axis=2)
            dot = jnp.sum(direction * direction) + jnp.sum(own_diag * own_state * own_state)
        if norm_now is None:
            sums = global_sum(jnp.stack([jnp.sum(residual * residual), dot]))
            norm_now, curvature = sums[0], sums[1]
        else:
            curvature = global_sum(dot)
        alpha = norm_now / curvature
        control = control + alpha * direction
        increment = increment + alpha * own_state
        if step + 1 < ITERS:
            residual = residual - alpha * image
            from_residual = forward(residual) if step + 2 == ITERS else None
            norm_next = global_sum(jnp.sum(residual * residual))
            beta = norm_next / norm_now
            direction = residual + beta * direction
            if from_residual is not None:
                ahead = (from_residual, beta, state)
            norm_now = norm_next
    control = to_output(control)
    increment = increment.transpose(0, 2, 1, 3).reshape(slots, lat_rows, shard_cols)
    return (control, increment)


def solution(mesh):
    return jax.shard_map(
        body,
        mesh=mesh,
        in_specs=(
            P("mem", None, "tile", None, None),
            P("tile", "mem"),
            P("tile", "mem"),
            P("tile", "mem"),
            P("tile"),
            P("tile"),
            P(),
            P(),
        ),
        out_specs=(P("mem", "tile", None, None), P(None, "tile", "mem")),
        check_vma=False,
    )
```

```python
import jax
import jax.numpy as jnp
from jax import lax
from jax.experimental import pallas as pl
from jax.experimental.pallas import tpu as pltpu
from jax.sharding import PartitionSpec as P

ITERS = 2
STEPS = 8


def row_mask(starts, lengths, nlon):
    lon = lax.broadcasted_iota(jnp.int32, (starts.shape[0], nlon), 1)
    rel = (lon - starts[:, None]) % nlon
    return jnp.where(rel < lengths[:, None], 1.0, 0.0).astype(jnp.float32)[:, None, :]


def diffuse_step(field, mask, lat_rate, lon_rate):
    zero = jnp.zeros_like(field[:, :1])
    north = jnp.concatenate([field[:, 1:], zero], axis=1)
    south = jnp.concatenate([zero, field[:, :-1]], axis=1)
    east = jnp.roll(field, -1, axis=3)
    west = jnp.roll(field, 1, axis=3)
    lat_term = north + south - 2.0 * field
    lon_term = east + west - 2.0 * field
    return mask * (
        field + lat_rate[:, None, None, None] * lat_term + lon_rate[:, None, None, None] * lon_term
    )


def smooth_level(rates_ref, mask, now, level):
    rows, members, nlon = now.shape
    lat = rates_ref[0, level]
    lon = rates_ref[1, level]
    zero = jnp.zeros((1, members, nlon), jnp.float32)
    now = mask * now
    for inner in range(STEPS):
        north = jnp.concatenate([now[1:], zero], axis=0)
        south = jnp.concatenate([zero, now[:-1]], axis=0)
        east = pltpu.roll(now, nlon - 1, 2)
        west = pltpu.roll(now, 1, 2)
        lat_term = north + south - 2.0 * now
        lon_term = east + west - 2.0 * now
        now = mask * (now + lat * lat_term + lon * lon_term)
    return now


def adjoint_kernel(rates_ref, mask_ref, pert_ref, diag_ref, state_ref, out_ref):
    slots, levels = pert_ref.shape[:2]
    mask = mask_ref[...]
    for level in range(levels):
        field = None
        for slot in range(slots):
            grad = diag_ref[slot, level] * state_ref[slot, level]
            term = pert_ref[slot, level] * grad[:, None, :]
            field = term if field is None else field + term
        out_ref[level] = smooth_level(rates_ref, mask, field, level)


def forward_kernel(rates_ref, mask_ref, pert_ref, field_ref, out_ref):
    slots, levels = pert_ref.shape[:2]
    mask = mask_ref[...]
    for level in range(levels):
        smoothed = smooth_level(rates_ref, mask, field_ref[level], level)
        for slot in range(slots):
            out_ref[slot, level] = jnp.sum(pert_ref[slot, level] * smoothed, axis=1)


def local_call(kernel, out_shape, rates, *arrays):
    size = sum(a.size for a in arrays)
    return pl.pallas_call(
        kernel,
        out_shape=jax.ShapeDtypeStruct(out_shape, jnp.float32),
        in_specs=[pl.BlockSpec(memory_space=pltpu.SMEM)]
        + [pl.BlockSpec(memory_space=pltpu.VMEM)] * len(arrays),
        out_specs=pl.BlockSpec(memory_space=pltpu.VMEM),
        cost_estimate=pl.CostEstimate(
            flops=16 * STEPS * size, bytes_accessed=4 * size, transcendentals=0
        ),
    )(rates, *arrays)


def global_sum(value):
    axes = ("tile", "mem")
    count = lax.axis_size(axes)
    value = jnp.asarray(value, jnp.float32)
    spread = jnp.broadcast_to(value, (count,) + value.shape)
    return jnp.sum(lax.all_to_all(spread, axes, 0, 0, tiled=True), axis=0)


def add_at_cells(cells, values, size):
    lanes = 128
    count, kinds = values.shape
    high = lax.broadcasted_iota(jnp.int32, (count, size // lanes), 1) == (cells // lanes)[:, None]
    low = lax.broadcasted_iota(jnp.int32, (count, lanes), 1) == (cells % lanes)[:, None]
    spread = values[:, :, None] * low.astype(jnp.float32)[:, None, :]
    summed = jnp.dot(
        high.astype(jnp.float32).T,
        spread.reshape(count, kinds * lanes),
        precision=lax.Precision.HIGHEST,
        preferred_element_type=jnp.float32,
    )
    return summed.reshape(size // lanes, kinds, lanes).transpose(0, 2, 1).reshape(size, kinds)


def gather_rows(block, dim):
    count = lax.axis_size("tile")
    shape = block.shape
    copies = jnp.broadcast_to(
        jnp.expand_dims(block, dim), shape[:dim] + (count,) + shape[dim:]
    )
    joined = lax.all_to_all(copies, "tile", dim, dim, tiled=True)
    return joined.reshape(shape[:dim] + (count * shape[dim],) + shape[dim + 1 :])


def gather_rows_by_permutes(block, dim):
    count = lax.axis_size("tile")
    me = lax.axis_index("tile")
    pieces = [block] + [
        lax.ppermute(block, "tile", [(i, (i + k) % count) for i in range(count)])
        for k in range(1, count)
    ]
    by_offset = jnp.stack([pieces[(count - q) % count] for q in range(count)], axis=dim)
    ordered = jnp.roll(by_offset, me, axis=dim)
    shape = block.shape
    return ordered.reshape(shape[:dim] + (count * shape[dim],) + shape[dim + 1 :])


def reduce_rows_by_permutes(block, dim):
    count = lax.axis_size("tile")
    me = lax.axis_index("tile")
    share = block.shape[dim] // count
    total = lax.dynamic_slice_in_dim(block, me * share, share, axis=dim)
    for k in range(1, count):
        piece = lax.dynamic_slice_in_dim(block, ((me + k) % count) * share, share, axis=dim)
        total = total + lax.ppermute(piece, "tile", [(i, (i + k) % count) for i in range(count)])
    return total


def sum_over_tile_by_permutes(block):
    count = lax.axis_size("tile")
    total = block
    for k in range(1, count):
        total = total + lax.ppermute(block, "tile", [(i, (i + k) % count) for i in range(count)])
    return total


def reduce_rows(block, dim):
    count = lax.axis_size("tile")
    shape = block.shape
    parts = block.reshape(shape[:dim] + (count, shape[dim] // count) + shape[dim + 1 :])
    received = lax.all_to_all(parts, "tile", dim, dim, tiled=True)
    return jnp.sum(received, axis=dim)


def body(
    perturbations, innovations, obs_weight, obs_cell, row_start, row_length, lat_rate, lon_rate
):
    slots = perturbations.shape[1]
    lat_rows = perturbations.shape[2]
    levels = perturbations.shape[3]
    nlon = perturbations.shape[4]
    groups = lax.axis_size("mem")
    own_levels = levels // groups
    shard_cols = own_levels * nlon
    first = lax.axis_index("mem") * own_levels
    lat_own = lax.dynamic_slice_in_dim(lat_rate, first, own_levels)
    lon_own = lax.dynamic_slice_in_dim(lon_rate, first, own_levels)

    tiles = lax.axis_size("tile")
    local_members = perturbations.shape[0]
    share = local_members // tiles
    if share and local_members % tiles == 0:
        sent = perturbations.astype(jnp.float32).reshape(
            tiles, share, slots, lat_rows, groups, own_levels, nlon
        )
        sent = sent.transpose(0, 4, 2, 5, 3, 1, 6).reshape(
            tiles * groups, slots, own_levels, lat_rows, share, nlon
        )
        got = lax.all_to_all(sent, ("tile", "mem"), 0, 0, tiled=True)
        pert = got.reshape(tiles, groups, slots, own_levels, lat_rows, share, nlon)
        pert = pert.transpose(2, 3, 0, 4, 1, 5, 6).reshape(
            slots, own_levels, tiles * lat_rows, groups * share, nlon
        )
    else:
        pert = lax.all_to_all(
            perturbations.astype(jnp.float32).transpose(1, 3, 2, 0, 4),
            "mem",
            split_axis=1,
            concat_axis=3,
            tiled=True,
        )
        pert = lax.all_to_all(pert, "tile", split_axis=3, concat_axis=2, tiled=True)

    rates = jnp.stack([lat_own, lon_own])

    def forward(control):
        partial = local_call(
            forward_kernel,
            (slots, own_levels, control.shape[1], nlon),
            rates,
            mask,
            pert,
            control,
        )
        return sum_over_tile_by_permutes(partial)

    def adjoint(diag, state):
        return local_call(
            adjoint_kernel, pert.shape[1:], rates, mask, pert, diag, state
        )

    def to_output(control):
        if share and local_members % tiles == 0:
            sent = control.reshape(own_levels, tiles, lat_rows, groups, share, nlon)
            sent = sent.transpose(1, 3, 0, 2, 4, 5).reshape(
                tiles * groups, own_levels, lat_rows, share, nlon
            )
            got = lax.all_to_all(sent, ("tile", "mem"), 0, 0, tiled=True)
            control = got.reshape(tiles, groups, own_levels, lat_rows, share, nlon)
            control = control.transpose(0, 4, 3, 1, 2, 5).reshape(
                tiles * share, lat_rows, levels, nlon
            )
        else:
            control = lax.all_to_all(control, "tile", split_axis=1, concat_axis=2, tiled=True)
            control = lax.all_to_all(control, "mem", split_axis=2, concat_axis=0, tiled=True)
            control = control.transpose(2, 1, 0, 3)
        return control

    local_cells = obs_cell[0]
    innov = innovations[0]
    weight = obs_weight[0]
    size = slots * lat_rows * shard_cols
    state_shape = (slots, own_levels, lat_rows, nlon)
    gathered = add_at_cells(local_cells, jnp.stack([weight * innov, weight], axis=1), size)
    gathered = gathered.reshape(slots, lat_rows, own_levels, nlon, 2).transpose(4, 0, 2, 1, 3)

    tables = jnp.zeros((lat_rows, nlon), jnp.float32)
    tables = tables.at[:, 0].set(row_start.astype(jnp.float32))
    tables = tables.at[:, 1].set(row_length.astype(jnp.float32))
    payload = jnp.concatenate(
        [gathered.reshape(2 * slots * own_levels, lat_rows, nlon), tables[None]], axis=0
    )
    payload = gather_rows_by_permutes(payload, 1)
    tables = payload[-1, :, :2].astype(jnp.int32)
    mask = row_mask(tables[:, 0], tables[:, 1], nlon)
    both = payload[:-1].reshape(2, slots, own_levels, tiles * lat_rows, nlon)
    first_grad, obs_diag = both[0], both[1]
    me = lax.axis_index("tile")

    residual = adjoint(first_grad, jnp.ones_like(first_grad))
    direction = residual
    control = jnp.zeros_like(residual)
    increment = jnp.zeros(state_shape, jnp.float32)
    norm_now = None
    ahead = None
    for step in range(ITERS):
        if ahead is None:
            state = forward(direction)
        else:
            state = ahead[0] + ahead[1] * ahead[2]
        own_state = lax.dynamic_slice_in_dim(state, me * lat_rows, lat_rows, axis=2)
        own_diag = lax.dynamic_slice_in_dim(obs_diag, me * lat_rows, lat_rows, axis=2)
        dot = jnp.sum(direction * direction) + jnp.sum(own_diag * own_state * own_state)
        if step + 1 < ITERS:
            image = direction + adjoint(obs_diag, state)
        if norm_now is None:
            sums = global_sum(jnp.stack([jnp.sum(residual * residual), dot]))
            norm_now, curvature = sums[0], sums[1]
        else:
            curvature = global_sum(dot)
        alpha = norm_now / curvature
        control = control + alpha * direction
        increment = increment + alpha * own_state
        if step + 1 < ITERS:
            residual = residual - alpha * image
            from_residual = forward(residual) if step + 2 == ITERS else None
            norm_next = global_sum(jnp.sum(residual * residual))
            beta = norm_next / norm_now
            direction = residual + beta * direction
            if from_residual is not None:
                ahead = (from_residual, beta, state)
            norm_now = norm_next
    control = to_output(control)
    increment = increment.transpose(0, 2, 1, 3).reshape(slots, lat_rows, shard_cols)
    return (control, increment)


def solution(mesh):
    return jax.shard_map(
        body,
        mesh=mesh,
        in_specs=(
            P("mem", None, "tile", None, None),
            P("tile", "mem"),
            P("tile", "mem"),
            P("tile", "mem"),
            P("tile"),
            P("tile"),
            P(),
            P(),
        ),
        out_specs=(P("mem", "tile", None, None), P(None, "tile", "mem")),
        check_vma=False,
    )
```

```python
import jax
import jax.numpy as jnp
from jax import lax
from jax.experimental import pallas as pl
from jax.experimental.pallas import tpu as pltpu
from jax.sharding import PartitionSpec as P

ITERS = 2
STEPS = 8


def row_mask(starts, lengths, nlon):
    lon = lax.broadcasted_iota(jnp.int32, (starts.shape[0], nlon), 1)
    rel = (lon - starts[:, None]) % nlon
    return jnp.where(rel < lengths[:, None], 1.0, 0.0).astype(jnp.float32)[:, None, :]


def diffuse_step(field, mask, lat_rate, lon_rate):
    zero = jnp.zeros_like(field[:, :1])
    north = jnp.concatenate([field[:, 1:], zero], axis=1)
    south = jnp.concatenate([zero, field[:, :-1]], axis=1)
    east = jnp.roll(field, -1, axis=3)
    west = jnp.roll(field, 1, axis=3)
    lat_term = north + south - 2.0 * field
    lon_term = east + west - 2.0 * field
    return mask * (
        field + lat_rate[:, None, None, None] * lat_term + lon_rate[:, None, None, None] * lon_term
    )


def smooth_level(rates_ref, mask, now, level):
    rows, members, nlon = now.shape
    lat = rates_ref[0, level]
    lon = rates_ref[1, level]
    zero = jnp.zeros((1, members, nlon), jnp.float32)
    now = mask * now
    for inner in range(STEPS):
        north = jnp.concatenate([now[1:], zero], axis=0)
        south = jnp.concatenate([zero, now[:-1]], axis=0)
        east = pltpu.roll(now, nlon - 1, 2)
        west = pltpu.roll(now, 1, 2)
        lat_term = north + south - 2.0 * now
        lon_term = east + west - 2.0 * now
        now = mask * (now + lat * lat_term + lon * lon_term)
    return now


def adjoint_kernel(rates_ref, mask_ref, pert_ref, diag_ref, state_ref, out_ref):
    slots, levels = pert_ref.shape[:2]
    mask = mask_ref[...]
    for level in range(levels):
        field = None
        for slot in range(slots):
            grad = diag_ref[slot, level] * state_ref[slot, level]
            term = pert_ref[slot, level] * grad[:, None, :]
            field = term if field is None else field + term
        out_ref[level] = smooth_level(rates_ref, mask, field, level)


def forward_kernel(rates_ref, mask_ref, pert_ref, field_ref, out_ref):
    slots, levels = pert_ref.shape[:2]
    mask = mask_ref[...]
    for level in range(levels):
        smoothed = smooth_level(rates_ref, mask, field_ref[level], level)
        for slot in range(slots):
            out_ref[slot, level] = jnp.sum(pert_ref[slot, level] * smoothed, axis=1)


def local_call(kernel, out_shape, rates, *arrays):
    size = sum(a.size for a in arrays)
    return pl.pallas_call(
        kernel,
        out_shape=jax.ShapeDtypeStruct(out_shape, jnp.float32),
        in_specs=[pl.BlockSpec(memory_space=pltpu.SMEM)]
        + [pl.BlockSpec(memory_space=pltpu.VMEM)] * len(arrays),
        out_specs=pl.BlockSpec(memory_space=pltpu.VMEM),
        cost_estimate=pl.CostEstimate(
            flops=16 * STEPS * size, bytes_accessed=4 * size, transcendentals=0
        ),
    )(rates, *arrays)


def global_sum(value):
    axes = ("tile", "mem")
    count = lax.axis_size(axes)
    value = jnp.asarray(value, jnp.float32)
    spread = jnp.broadcast_to(value, (count,) + value.shape)
    return jnp.sum(lax.all_to_all(spread, axes, 0, 0, tiled=True), axis=0)


def add_at_cells(cells, values, size):
    lanes = 128
    count, kinds = values.shape
    high = lax.broadcasted_iota(jnp.int32, (count, size // lanes), 1) == (cells // lanes)[:, None]
    low = lax.broadcasted_iota(jnp.int32, (count, lanes), 1) == (cells % lanes)[:, None]
    spread = values[:, :, None] * low.astype(jnp.float32)[:, None, :]
    summed = jnp.dot(
        high.astype(jnp.float32).T,
        spread.reshape(count, kinds * lanes),
        precision=lax.Precision.HIGHEST,
        preferred_element_type=jnp.float32,
    )
    return summed.reshape(size // lanes, kinds, lanes).transpose(0, 2, 1).reshape(size, kinds)


def gather_rows(block, dim):
    count = lax.axis_size("tile")
    shape = block.shape
    copies = jnp.broadcast_to(
        jnp.expand_dims(block, dim), shape[:dim] + (count,) + shape[dim:]
    )
    joined = lax.all_to_all(copies, "tile", dim, dim, tiled=True)
    return joined.reshape(shape[:dim] + (count * shape[dim],) + shape[dim + 1 :])


def gather_rows_by_permutes(block, dim):
    count = lax.axis_size("tile")
    me = lax.axis_index("tile")
    pieces = [block] + [
        lax.ppermute(block, "tile", [(i, (i + k) % count) for i in range(count)])
        for k in range(1, count)
    ]
    by_offset = jnp.stack([pieces[(count - q) % count] for q in range(count)], axis=dim)
    ordered = jnp.roll(by_offset, me, axis=dim)
    shape = block.shape
    return ordered.reshape(shape[:dim] + (count * shape[dim],) + shape[dim + 1 :])


def reduce_rows_by_permutes(block, dim):
    count = lax.axis_size("tile")
    me = lax.axis_index("tile")
    share = block.shape[dim] // count
    total = lax.dynamic_slice_in_dim(block, me * share, share, axis=dim)
    for k in range(1, count):
        piece = lax.dynamic_slice_in_dim(block, ((me + k) % count) * share, share, axis=dim)
        total = total + lax.ppermute(piece, "tile", [(i, (i + k) % count) for i in range(count)])
    return total


def sum_over_tile_by_permutes(block):
    count = lax.axis_size("tile")
    total = block
    for k in range(1, count):
        total = total + lax.ppermute(block, "tile", [(i, (i + k) % count) for i in range(count)])
    return total


def reduce_rows(block, dim):
    count = lax.axis_size("tile")
    shape = block.shape
    parts = block.reshape(shape[:dim] + (count, shape[dim] // count) + shape[dim + 1 :])
    received = lax.all_to_all(parts, "tile", dim, dim, tiled=True)
    return jnp.sum(received, axis=dim)


def body(
    perturbations, innovations, obs_weight, obs_cell, row_start, row_length, lat_rate, lon_rate
):
    slots = perturbations.shape[1]
    lat_rows = perturbations.shape[2]
    levels = perturbations.shape[3]
    nlon = perturbations.shape[4]
    groups = lax.axis_size("mem")
    own_levels = levels // groups
    shard_cols = own_levels * nlon
    first = lax.axis_index("mem") * own_levels
    lat_own = lax.dynamic_slice_in_dim(lat_rate, first, own_levels)
    lon_own = lax.dynamic_slice_in_dim(lon_rate, first, own_levels)

    tiles = lax.axis_size("tile")
    local_members = perturbations.shape[0]
    share = local_members // tiles
    if share and local_members % tiles == 0:
        sent = perturbations.astype(jnp.float32).reshape(
            tiles, share, slots, lat_rows, groups, own_levels, nlon
        )
        sent = sent.transpose(0, 4, 2, 5, 3, 1, 6).reshape(
            tiles * groups, slots, own_levels, lat_rows, share, nlon
        )
        got = lax.all_to_all(sent, ("tile", "mem"), 0, 0, tiled=True)
        pert = got.reshape(tiles, groups, slots, own_levels, lat_rows, share, nlon)
        pert = pert.transpose(2, 3, 0, 4, 1, 5, 6).reshape(
            slots, own_levels, tiles * lat_rows, groups * share, nlon
        )
    else:
        pert = lax.all_to_all(
            perturbations.astype(jnp.float32).transpose(1, 3, 2, 0, 4),
            "mem",
            split_axis=1,
            concat_axis=3,
            tiled=True,
        )
        pert = lax.all_to_all(pert, "tile", split_axis=3, concat_axis=2, tiled=True)

    rates = jnp.stack([lat_own, lon_own])

    def forward(control, own_rows=False):
        partial = local_call(
            forward_kernel,
            (slots, own_levels, control.shape[1], nlon),
            rates,
            mask,
            pert,
            control,
        )
        if own_rows:
            return reduce_rows_by_permutes(partial, 2)
        return sum_over_tile_by_permutes(partial)

    def adjoint(diag, state):
        return local_call(
            adjoint_kernel, pert.shape[1:], rates, mask, pert, diag, state
        )

    def to_output(control):
        if share and local_members % tiles == 0:
            sent = control.reshape(own_levels, tiles, lat_rows, groups, share, nlon)
            sent = sent.transpose(1, 3, 0, 2, 4, 5).reshape(
                tiles * groups, own_levels, lat_rows, share, nlon
            )
            got = lax.all_to_all(sent, ("tile", "mem"), 0, 0, tiled=True)
            control = got.reshape(tiles, groups, own_levels, lat_rows, share, nlon)
            control = control.transpose(0, 4, 3, 1, 2, 5).reshape(
                tiles * share, lat_rows, levels, nlon
            )
        else:
            control = lax.all_to_all(control, "tile", split_axis=1, concat_axis=2, tiled=True)
            control = lax.all_to_all(control, "mem", split_axis=2, concat_axis=0, tiled=True)
            control = control.transpose(2, 1, 0, 3)
        return control

    local_cells = obs_cell[0]
    innov = innovations[0]
    weight = obs_weight[0]
    size = slots * lat_rows * shard_cols
    state_shape = (slots, own_levels, lat_rows, nlon)
    gathered = add_at_cells(local_cells, jnp.stack([weight * innov, weight], axis=1), size)
    gathered = gathered.reshape(slots, lat_rows, own_levels, nlon, 2).transpose(4, 0, 2, 1, 3)

    tables = jnp.zeros((lat_rows, nlon), jnp.float32)
    tables = tables.at[:, 0].set(row_start.astype(jnp.float32))
    tables = tables.at[:, 1].set(row_length.astype(jnp.float32))
    payload = jnp.concatenate(
        [gathered.reshape(2 * slots * own_levels, lat_rows, nlon), tables[None]], axis=0
    )
    payload = gather_rows_by_permutes(payload, 1)
    tables = payload[-1, :, :2].astype(jnp.int32)
    mask = row_mask(tables[:, 0], tables[:, 1], nlon)
    both = payload[:-1].reshape(2, slots, own_levels, tiles * lat_rows, nlon)
    first_grad, obs_diag = both[0], both[1]
    me = lax.axis_index("tile")

    residual = adjoint(first_grad, jnp.ones_like(first_grad))
    direction = residual
    control = jnp.zeros_like(residual)
    increment = jnp.zeros(state_shape, jnp.float32)
    norm_now = None
    ahead = None
    for step in range(ITERS):
        if ahead is None:
            state = forward(direction)
        else:
            state = None
            own_state = ahead[0] + ahead[1] * ahead[2]
        if state is not None:
            own_state = lax.dynamic_slice_in_dim(state, me * lat_rows, lat_rows, axis=2)
        own_diag = lax.dynamic_slice_in_dim(obs_diag, me * lat_rows, lat_rows, axis=2)
        dot = jnp.sum(direction * direction) + jnp.sum(own_diag * own_state * own_state)
        if step + 1 < ITERS:
            image = direction + adjoint(obs_diag, state)
        if norm_now is None:
            sums = global_sum(jnp.stack([jnp.sum(residual * residual), dot]))
            norm_now, curvature = sums[0], sums[1]
        else:
            curvature = global_sum(dot)
        alpha = norm_now / curvature
        control = control + alpha * direction
        increment = increment + alpha * own_state
        if step + 1 < ITERS:
            residual = residual - alpha * image
            from_residual = forward(residual, own_rows=True) if step + 2 == ITERS else None
            norm_next = global_sum(jnp.sum(residual * residual))
            beta = norm_next / norm_now
            direction = residual + beta * direction
            if from_residual is not None:
                ahead = (from_residual, beta, own_state)
            norm_now = norm_next
    control = to_output(control)
    increment = increment.transpose(0, 2, 1, 3).reshape(slots, lat_rows, shard_cols)
    return (control, increment)


def solution(mesh):
    return jax.shard_map(
        body,
        mesh=mesh,
        in_specs=(
            P("mem", None, "tile", None, None),
            P("tile", "mem"),
            P("tile", "mem"),
            P("tile", "mem"),
            P("tile"),
            P("tile"),
            P(),
            P(),
        ),
        out_specs=(P("mem", "tile", None, None), P(None, "tile", "mem")),
        check_vma=False,
    )
```

```python
import jax
import jax.numpy as jnp
from jax import lax
from jax.experimental import pallas as pl
from jax.experimental.pallas import tpu as pltpu
from jax.sharding import PartitionSpec as P

ITERS = 2
STEPS = 8


def row_mask(starts, lengths, nlon):
    lon = lax.broadcasted_iota(jnp.int32, (starts.shape[0], nlon), 1)
    rel = (lon - starts[:, None]) % nlon
    return jnp.where(rel < lengths[:, None], 1.0, 0.0).astype(jnp.float32)[:, None, :]


def diffuse_step(field, mask, lat_rate, lon_rate):
    zero = jnp.zeros_like(field[:, :1])
    north = jnp.concatenate([field[:, 1:], zero], axis=1)
    south = jnp.concatenate([zero, field[:, :-1]], axis=1)
    east = jnp.roll(field, -1, axis=3)
    west = jnp.roll(field, 1, axis=3)
    lat_term = north + south - 2.0 * field
    lon_term = east + west - 2.0 * field
    return mask * (
        field + lat_rate[:, None, None, None] * lat_term + lon_rate[:, None, None, None] * lon_term
    )


def smooth_level(rates_ref, mask, now, level):
    rows, members, nlon = now.shape
    lat = rates_ref[0, level]
    lon = rates_ref[1, level]
    zero = jnp.zeros((1, members, nlon), jnp.float32)
    now = mask * now
    for inner in range(STEPS):
        north = jnp.concatenate([now[1:], zero], axis=0)
        south = jnp.concatenate([zero, now[:-1]], axis=0)
        east = pltpu.roll(now, nlon - 1, 2)
        west = pltpu.roll(now, 1, 2)
        lat_term = north + south - 2.0 * now
        lon_term = east + west - 2.0 * now
        now = mask * (now + lat * lat_term + lon * lon_term)
    return now


def adjoint_kernel(rates_ref, mask_ref, pert_ref, diag_ref, *refs):
    state_refs, out_ref = refs[:-1], refs[-1]
    slots, levels = pert_ref.shape[:2]
    mask = mask_ref[...]
    for level in range(levels):
        field = None
        for slot in range(slots):
            grad = diag_ref[slot, level]
            if state_refs:
                grad = grad * state_refs[0][slot, level]
            term = pert_ref[slot, level] * grad[:, None, :]
            field = term if field is None else field + term
        out_ref[level] = smooth_level(rates_ref, mask, field, level)


def forward_kernel(rates_ref, mask_ref, pert_ref, field_ref, out_ref):
    slots, levels = pert_ref.shape[:2]
    mask = mask_ref[...]
    for level in range(levels):
        smoothed = smooth_level(rates_ref, mask, field_ref[level], level)
        for slot in range(slots):
            out_ref[slot, level] = jnp.sum(pert_ref[slot, level] * smoothed, axis=1)


def local_call(kernel, out_shape, rates, *arrays):
    size = sum(a.size for a in arrays)
    return pl.pallas_call(
        kernel,
        out_shape=jax.ShapeDtypeStruct(out_shape, jnp.float32),
        in_specs=[pl.BlockSpec(memory_space=pltpu.SMEM)]
        + [pl.BlockSpec(memory_space=pltpu.VMEM)] * len(arrays),
        out_specs=pl.BlockSpec(memory_space=pltpu.VMEM),
        cost_estimate=pl.CostEstimate(
            flops=16 * STEPS * size, bytes_accessed=4 * size, transcendentals=0
        ),
    )(rates, *arrays)


def global_sum(value):
    axes = ("tile", "mem")
    count = lax.axis_size(axes)
    value = jnp.asarray(value, jnp.float32)
    spread = jnp.broadcast_to(value, (count,) + value.shape)
    return jnp.sum(lax.all_to_all(spread, axes, 0, 0, tiled=True), axis=0)


def add_at_cells(cells, values, size):
    lanes = 128
    count, kinds = values.shape
    high = lax.broadcasted_iota(jnp.int32, (count, size // lanes), 1) == (cells // lanes)[:, None]
    low = lax.broadcasted_iota(jnp.int32, (count, lanes), 1) == (cells % lanes)[:, None]
    spread = values[:, :, None] * low.astype(jnp.float32)[:, None, :]
    summed = jnp.dot(
        high.astype(jnp.float32).T,
        spread.reshape(count, kinds * lanes),
        precision=lax.Precision.HIGHEST,
        preferred_element_type=jnp.float32,
    )
    return summed.reshape(size // lanes, kinds, lanes).transpose(0, 2, 1).reshape(size, kinds)


def gather_rows(block, dim):
    count = lax.axis_size("tile")
    shape = block.shape
    copies = jnp.broadcast_to(
        jnp.expand_dims(block, dim), shape[:dim] + (count,) + shape[dim:]
    )
    joined = lax.all_to_all(copies, "tile", dim, dim, tiled=True)
    return joined.reshape(shape[:dim] + (count * shape[dim],) + shape[dim + 1 :])


def gather_rows_by_permutes(block, dim):
    count = lax.axis_size("tile")
    me = lax.axis_index("tile")
    pieces = [block] + [
        lax.ppermute(block, "tile", [(i, (i + k) % count) for i in range(count)])
        for k in range(1, count)
    ]
    by_offset = jnp.stack([pieces[(count - q) % count] for q in range(count)], axis=dim)
    ordered = jnp.roll(by_offset, me, axis=dim)
    shape = block.shape
    return ordered.reshape(shape[:dim] + (count * shape[dim],) + shape[dim + 1 :])


def reduce_rows_by_permutes(block, dim):
    count = lax.axis_size("tile")
    me = lax.axis_index("tile")
    share = block.shape[dim] // count
    total = lax.dynamic_slice_in_dim(block, me * share, share, axis=dim)
    for k in range(1, count):
        piece = lax.dynamic_slice_in_dim(block, ((me + k) % count) * share, share, axis=dim)
        total = total + lax.ppermute(piece, "tile", [(i, (i + k) % count) for i in range(count)])
    return total


def sum_over_tile_by_permutes(block):
    count = lax.axis_size("tile")
    total = block
    for k in range(1, count):
        total = total + lax.ppermute(block, "tile", [(i, (i + k) % count) for i in range(count)])
    return total


def reduce_rows(block, dim):
    count = lax.axis_size("tile")
    shape = block.shape
    parts = block.reshape(shape[:dim] + (count, shape[dim] // count) + shape[dim + 1 :])
    received = lax.all_to_all(parts, "tile", dim, dim, tiled=True)
    return jnp.sum(received, axis=dim)


def body(
    perturbations, innovations, obs_weight, obs_cell, row_start, row_length, lat_rate, lon_rate
):
    slots = perturbations.shape[1]
    lat_rows = perturbations.shape[2]
    levels = perturbations.shape[3]
    nlon = perturbations.shape[4]
    groups = lax.axis_size("mem")
    own_levels = levels // groups
    shard_cols = own_levels * nlon
    first = lax.axis_index("mem") * own_levels
    lat_own = lax.dynamic_slice_in_dim(lat_rate, first, own_levels)
    lon_own = lax.dynamic_slice_in_dim(lon_rate, first, own_levels)

    tiles = lax.axis_size("tile")
    local_members = perturbations.shape[0]
    share = local_members // tiles
    if share and local_members % tiles == 0:
        sent = perturbations.astype(jnp.float32).reshape(
            tiles, share, slots, lat_rows, groups, own_levels, nlon
        )
        sent = sent.transpose(0, 4, 2, 5, 3, 1, 6).reshape(
            tiles * groups, slots, own_levels, lat_rows, share, nlon
        )
        got = lax.all_to_all(sent, ("tile", "mem"), 0, 0, tiled=True)
        pert = got.reshape(tiles, groups, slots, own_levels, lat_rows, share, nlon)
        pert = pert.transpose(2, 3, 0, 4, 1, 5, 6).reshape(
            slots, own_levels, tiles * lat_rows, groups * share, nlon
        )
    else:
        pert = lax.all_to_all(
            perturbations.astype(jnp.float32).transpose(1, 3, 2, 0, 4),
            "mem",
            split_axis=1,
            concat_axis=3,
            tiled=True,
        )
        pert = lax.all_to_all(pert, "tile", split_axis=3, concat_axis=2, tiled=True)

    rates = jnp.stack([lat_own, lon_own])

    def forward(control, own_rows=False):
        partial = local_call(
            forward_kernel,
            (slots, own_levels, control.shape[1], nlon),
            rates,
            mask,
            pert,
            control,
        )
        if own_rows:
            return reduce_rows_by_permutes(partial, 2)
        return sum_over_tile_by_permutes(partial)

    def adjoint(diag, state):
        states = () if state is None else (state,)
        return local_call(adjoint_kernel, pert.shape[1:], rates, mask, pert, diag, *states)

    def to_output(control):
        if share and local_members % tiles == 0:
            sent = control.reshape(own_levels, tiles, lat_rows, groups, share, nlon)
            sent = sent.transpose(1, 3, 0, 2, 4, 5).reshape(
                tiles * groups, own_levels, lat_rows, share, nlon
            )
            got = lax.all_to_all(sent, ("tile", "mem"), 0, 0, tiled=True)
            control = got.reshape(tiles, groups, own_levels, lat_rows, share, nlon)
            control = control.transpose(0, 4, 3, 1, 2, 5).reshape(
                tiles * share, lat_rows, levels, nlon
            )
        else:
            control = lax.all_to_all(control, "tile", split_axis=1, concat_axis=2, tiled=True)
            control = lax.all_to_all(control, "mem", split_axis=2, concat_axis=0, tiled=True)
            control = control.transpose(2, 1, 0, 3)
        return control

    local_cells = obs_cell[0]
    innov = innovations[0]
    weight = obs_weight[0]
    size = slots * lat_rows * shard_cols
    state_shape = (slots, own_levels, lat_rows, nlon)
    gathered = add_at_cells(local_cells, jnp.stack([weight * innov, weight], axis=1), size)
    gathered = gathered.reshape(slots, lat_rows, own_levels, nlon, 2).transpose(4, 0, 2, 1, 3)

    tables = jnp.zeros((lat_rows, nlon), jnp.float32)
    tables = tables.at[:, 0].set(row_start.astype(jnp.float32))
    tables = tables.at[:, 1].set(row_length.astype(jnp.float32))
    payload = jnp.concatenate(
        [gathered.reshape(2 * slots * own_levels, lat_rows, nlon), tables[None]], axis=0
    )
    payload = gather_rows_by_permutes(payload, 1)
    tables = payload[-1, :, :2].astype(jnp.int32)
    mask = row_mask(tables[:, 0], tables[:, 1], nlon)
    both = payload[:-1].reshape(2, slots, own_levels, tiles * lat_rows, nlon)
    first_grad, obs_diag = both[0], both[1]
    me = lax.axis_index("tile")

    residual = adjoint(first_grad, None)
    direction = residual
    control = jnp.zeros_like(residual)
    increment = jnp.zeros(state_shape, jnp.float32)
    norm_now = None
    ahead = None
    for step in range(ITERS):
        if ahead is None:
            state = forward(direction)
        else:
            state = None
            own_state = ahead[0] + ahead[1] * ahead[2]
        if state is not None:
            own_state = lax.dynamic_slice_in_dim(state, me * lat_rows, lat_rows, axis=2)
        own_diag = lax.dynamic_slice_in_dim(obs_diag, me * lat_rows, lat_rows, axis=2)
        dot = jnp.sum(direction * direction) + jnp.sum(own_diag * own_state * own_state)
        if step + 1 < ITERS:
            image = direction + adjoint(obs_diag, state)
        if norm_now is None:
            sums = global_sum(jnp.stack([jnp.sum(residual * residual), dot]))
            norm_now, curvature = sums[0], sums[1]
        else:
            curvature = global_sum(dot)
        alpha = norm_now / curvature
        control = control + alpha * direction
        increment = increment + alpha * own_state
        if step + 1 < ITERS:
            residual = residual - alpha * image
            from_residual = forward(residual, own_rows=True) if step + 2 == ITERS else None
            norm_next = global_sum(jnp.sum(residual * residual))
            beta = norm_next / norm_now
            direction = residual + beta * direction
            if from_residual is not None:
                ahead = (from_residual, beta, own_state)
            norm_now = norm_next
    control = to_output(control)
    increment = increment.transpose(0, 2, 1, 3).reshape(slots, lat_rows, shard_cols)
    return (control, increment)


def solution(mesh):
    return jax.shard_map(
        body,
        mesh=mesh,
        in_specs=(
            P("mem", None, "tile", None, None),
            P("tile", "mem"),
            P("tile", "mem"),
            P("tile", "mem"),
            P("tile"),
            P("tile"),
            P(),
            P(),
        ),
        out_specs=(P("mem", "tile", None, None), P(None, "tile", "mem")),
        check_vma=False,
    )
```
